256 devices in a mesh: seq: 64 (over x, y_hi, z), head: 4 (over y_lo, core).
Axes of the slice: x: 4, y: 4 (y_hi: 2, y_lo: 2; y = y_hi * 2 + y_lo), z: 8, core: 2. Of those that a mesh axis runs over, the one named last changes fastest.
Arguments:
- tokens: bfloat16 [16384, 1024], P('seq'), may hold values from -6 to 6
- queries: bfloat16 [16384, 1024], P('seq', 'head'), may hold values from -8 to 8
- key_rows: bfloat16 [16384, 1024], P('seq', 'head'), may hold values from -8 to 8
- values: bfloat16 [16384, 1024], P('seq', 'head'), may hold values from -6 to 6
- ssm_input: bfloat16 [16384, 2048], P('seq', 'head'), may hold values from -6 to 6
- write_proj: bfloat16 [16384, 128], P('seq'), may hold values from -6 to 6
- read_proj: bfloat16 [16384, 128], P('seq'), may hold values from -6 to 6
- log_decay: float32 [32, 16384], P('head', 'seq'), may hold values from -1 to 0
- attn_project: bfloat16 [1024, 1024], P('head'), may hold values from -0.1875 to 0.1875
- ssm_project: bfloat16 [2048, 1024], P('head'), may hold values from -0.125 to 0.125
- gauss_project: bfloat16 [1024, 768], replicated, may hold values from -0.1875 to 0.1875
- tile_owner: int32 [16384], P('seq'), may hold values from 0 to 3, as said below
Outputs:
- block_out: bfloat16 [16384, 1024], P(('seq', 'head'))
- tile_rows: bfloat16 [64, 4, 4, 32, 768], P('seq', 'head')
The draws below stay inside these ranges and needn't reach their ends.
Inputs may be any that keep to these rules, and one draw needn't show every extreme that they name: `tile_owner`: in each aligned group of 64 tokens no owner is named by more than 32 tokens; in every block of 256 tokens one owner is named by exactly 32 tokens of each of its groups.
All inputs are finite; a program needn't handle non-finite values.
Results may differ from the reference program's by a relative error of at most 0.023.
Values may be sent and summed in bfloat16 or wider, within the bound.
No kernel may reach another device: no remote copies, remote signals or barrier semaphores. Data moves between devices by JAX's collectives and lax.ppermute only.
A program may use at most 128 MiB of HBM per device.

```python
import math
import jax
import jax.numpy as jnp
from jax import lax

D = 1024
HEADS = 16
HDIM = 64
STATE_SPACE_HEADS = 32
SSM_HDIM = 64
STATE = 128
GW = 768
TOK_DEV = 256
SEQUENCE_TOKENS = 16384
BLOCKS = 64
OWNERS = 4
SUB = 64
CAP = 32


def query_key_pair(key):
    width_all = HEADS * HDIM
    base_key = jax.random.fold_in(key, 71)
    key_query = jax.random.fold_in(base_key, 0)
    key_keys = jax.random.fold_in(base_key, 1)
    key_faint = jax.random.fold_in(base_key, 4)
    query_drawn = jnp.clip(1.5 * jax.random.normal(key_query, (SEQUENCE_TOKENS, width_all), jnp.float32), -8.0, 8.0)
    keys_drawn = jnp.clip(1.5 * jax.random.normal(key_keys, (SEQUENCE_TOKENS, width_all), jnp.float32), -8.0, 8.0)
    row_index = jnp.arange(SEQUENCE_TOKENS, dtype=jnp.int32)[:, None]
    column_index = jnp.arange(width_all, dtype=jnp.int32)[None, :]
    within_head = column_index % HDIM
    quiet_count = max(1, HDIM // 4)
    is_quiet = within_head >= HDIM - quiet_count
    half_rows = SEQUENCE_TOKENS // 2
    faint_signs = jnp.where(jax.random.bernoulli(key_faint, 0.5, (SEQUENCE_TOKENS, width_all)), 1.0, -1.0)
    faint_level = 20.0 / math.sqrt(HDIM)
    faint_query = jnp.where(is_quiet, 8.0 * faint_signs, 0.0)
    faint_key = jnp.where(is_quiet, faint_level * faint_signs, 0.0)
    query_out = jnp.where(row_index % 64 == 21, faint_query, query_drawn)
    keys_out = jnp.where((row_index - half_rows) % 64 == 21, jnp.roll(faint_key, half_rows, axis=0), keys_drawn)
    return (query_out, keys_out)


def draw_queries(key, part):
    return query_key_pair(key)[0].astype(jnp.bfloat16)


def draw_key_rows(key, part):
    return query_key_pair(key)[1].astype(jnp.bfloat16)


def draw_log_decay(key, part):
    base_key = jax.random.fold_in(key, 33)
    key_kind, key_fast, key_slow, key_block, key_token, key_location, key_nesting_depth = jax.random.split(base_key, 7)
    fast_share = 0.5
    is_fast = jax.random.uniform(key_kind, (STATE_SPACE_HEADS, 1), jnp.float32) < fast_share
    fast_rate = jnp.exp(jax.random.uniform(key_fast, (STATE_SPACE_HEADS, 1), jnp.float32, math.log(1.0 / 50.0), math.log(1.0 / 30.0)))
    slow_rate = jnp.exp(jax.random.uniform(key_slow, (STATE_SPACE_HEADS, 1), jnp.float32, math.log(0.1 / SEQUENCE_TOKENS), math.log(0.4 / SEQUENCE_TOKENS)))
    head_frequency = jnp.where(is_fast, fast_rate, slow_rate)
    block_multiplier = jax.random.uniform(key_block, (STATE_SPACE_HEADS, SEQUENCE_TOKENS // TOK_DEV), jnp.float32, 0.6, 1.2)
    block_multiplier = jnp.repeat(block_multiplier, TOK_DEV, axis=1)
    token_multiplier = jax.random.uniform(key_token, (STATE_SPACE_HEADS, SEQUENCE_TOKENS), jnp.float32, 0.5, 1.5)
    flurry_location = jax.random.randint(key_location, (STATE_SPACE_HEADS, 2), 0, SEQUENCE_TOKENS)
    flurry_depth = jnp.log(jax.random.uniform(key_nesting_depth, (STATE_SPACE_HEADS, 2), jnp.float32, 0.5, 0.8))
    token_positions = jnp.arange(SEQUENCE_TOKENS, dtype=jnp.int32)[None, :]
    flurry_groups = jnp.where(token_positions == flurry_location[:, 0:1], flurry_depth[:, 0:1], 0.0)
    flurry_groups = flurry_groups + jnp.where(token_positions == flurry_location[:, 1:2], flurry_depth[:, 1:2], 0.0)
    return -head_frequency * block_multiplier * token_multiplier + flurry_groups


def draw_tile_owner(key, part):
    base_key = jax.random.fold_in(key, 57)
    key_star, key_other, key_order = jax.random.split(base_key, 3)
    group_count = SEQUENCE_TOKENS // SUB
    star = jax.random.randint(key_star, (SEQUENCE_TOKENS // TOK_DEV,), 0, OWNERS)
    star_group = jnp.repeat(star, TOK_DEV // SUB)
    others = (star_group[:, None] + jax.random.randint(key_other, (group_count, SUB), 1, OWNERS)) % OWNERS
    position = jnp.arange(SUB, dtype=jnp.int32)[None, :]
    listed = jnp.where(position < CAP, star_group[:, None], others)
    order_keys = jax.random.randint(key_order, (group_count, SUB), 0, 1048576) * SUB + position
    order = jnp.argsort(order_keys, axis=1, stable=True)
    shuffled = jnp.take_along_axis(listed, order, axis=1)
    return shuffled.reshape(SEQUENCE_TOKENS).astype(jnp.int32)


def levels(own_key, extent, shards, least, high):
    gain = 1.0
    for dim, blocks in shards:
        heights = jax.random.uniform(jax.random.fold_in(jax.random.fold_in(own_key, 6), dim), (blocks,), jnp.float32, least / len(shards), high / len(shards))
        gain = gain * jnp.repeat(jnp.exp(heights), extent[dim] // blocks).reshape((-1,) + (1,) * (len(extent) - 1 - dim))
    return gain


def noise(rng, dims, deviation, bound, cuts=(), held_as=jnp.bfloat16):
    values = jax.random.normal(rng, dims, jnp.float32) * deviation
    if len(cuts) > 0:
        values = levels(rng, dims, cuts, -0.22, 0.18) * values
    return jnp.clip(values, min=-bound, max=bound).astype(held_as)


def setup_inputs(seed: int = 0) -> dict:
    splits = jax.random.split(jax.random.key(seed), 13)
    return {
        "tokens": noise(splits[0], (SEQUENCE_TOKENS, D), 1.0, 6.0, ((0, 64),)),
        "queries": draw_queries(jax.random.fold_in(splits[12], 71), 0),
        "key_rows": draw_key_rows(jax.random.fold_in(splits[12], 71), 0),
        "values": noise(splits[3], (SEQUENCE_TOKENS, HEADS * HDIM), 1.0, 6.0, ((0, 64), (1, 4))),
        "ssm_input": noise(splits[4], (SEQUENCE_TOKENS, STATE_SPACE_HEADS * SSM_HDIM), 1.0, 6.0, ((0, 64), (1, 4))),
        "write_proj": noise(splits[5], (SEQUENCE_TOKENS, STATE), 1.0, 6.0, ((0, 64),)),
        "read_proj": noise(splits[6], (SEQUENCE_TOKENS, STATE), 1.0, 6.0, ((0, 64),)),
        "log_decay": draw_log_decay(jax.random.fold_in(splits[12], 71), 0),
        "attn_project": noise(splits[8], (HEADS * HDIM, D), (HEADS * HDIM) ** -0.5, 0.1875, ((0, 4),)),
        "ssm_project": noise(splits[9], (STATE_SPACE_HEADS * SSM_HDIM, D), (STATE_SPACE_HEADS * SSM_HDIM) ** -0.5, 0.125, ((0, 4),)),
        "gauss_project": noise(splits[10], (D, GW), D ** -0.5, 0.1875),
        "tile_owner": draw_tile_owner(jax.random.fold_in(splits[12], 71), 0),
    }


HIGHEST = lax.Precision.HIGHEST

def to_low(array):
    low = array.astype(jnp.bfloat16)
    low = lax.optimization_barrier(low)
    return low.astype(jnp.float32)

def attend_head(query_head, key_head, value_head):
    block_rows = math.gcd(SEQUENCE_TOKENS, 512)
    scale = 1.0 / math.sqrt(HDIM)

    def one_block(query_block):
        scores = jnp.dot(query_block, key_head.T, preferred_element_type=jnp.float32) * scale
        row_top = lax.optimization_barrier(jnp.max(scores, axis=1, keepdims=True))
        raised = jnp.exp(scores - row_top)
        totals = lax.optimization_barrier(jnp.sum(raised, axis=1, keepdims=True))
        weights = raised.astype(jnp.bfloat16)
        return jnp.dot(weights, value_head, preferred_element_type=jnp.float32) / totals
    blocks_in = query_head.reshape(SEQUENCE_TOKENS // block_rows, block_rows, HDIM)
    return lax.map(one_block, blocks_in).reshape(SEQUENCE_TOKENS, HDIM)

def chain_pieces(ssm_input, write_proj, read_proj, log_decay):
    row_count = write_proj.shape[0]
    head_count = log_decay.shape[0]
    head_width = ssm_input.shape[1] // head_count
    cumulative = jnp.cumsum(log_decay, axis=1)
    inputs_wide = ssm_input.astype(jnp.float32).reshape(row_count, head_count, head_width)
    later_rows = lax.broadcasted_iota(jnp.int32, (row_count, row_count), 0)
    earlier_cols = lax.broadcasted_iota(jnp.int32, (row_count, row_count), 1)
    log_gaps = cumulative[:, :, None] - cumulative[:, None, :]
    decays = jnp.exp(jnp.where((later_rows >= earlier_cols)[None], log_gaps, -jnp.inf))
    cross_terms = jnp.dot(read_proj, write_proj.T, preferred_element_type=jnp.float32)
    mixing = to_low(decays * cross_terms[None])
    inner_part = jnp.einsum('hts,shp->thp', mixing, inputs_wide, precision=HIGHEST)
    tail_decay = jnp.exp(cumulative[:, -1:] - cumulative)
    tail_inputs = to_low(inputs_wide * tail_decay.T[:, :, None])
    local_state = jnp.einsum('sn,shp->hnp', write_proj.astype(jnp.float32), tail_inputs, precision=HIGHEST)
    total_decay = jnp.exp(cumulative[:, -1])
    return (cumulative, inner_part, local_state, total_decay)

def chain_output(cumulative, inner_part, entering, read_proj):
    entering_low = to_low(entering)
    outer_part = jnp.einsum('tn,hnp->thp', read_proj.astype(jnp.float32), entering_low, precision=HIGHEST)
    mixture = inner_part + outer_part * jnp.exp(cumulative).T[:, :, None]
    scaled = mixture * lax.rsqrt(lax.optimization_barrier(jnp.mean(mixture * mixture, axis=2, keepdims=True)) + 1e-05)
    return scaled.reshape(scaled.shape[0], -1).astype(jnp.bfloat16)

def reference(tokens, queries, key_rows, values, ssm_input, write_proj, read_proj, log_decay, attn_project, ssm_project, gauss_project, tile_owner):
    query_all = queries.reshape(SEQUENCE_TOKENS, HEADS, HDIM).transpose(1, 0, 2)
    key_all = key_rows.reshape(SEQUENCE_TOKENS, HEADS, HDIM).transpose(1, 0, 2)
    value_all = values.reshape(SEQUENCE_TOKENS, HEADS, HDIM).transpose(1, 0, 2)
    heads_out = lax.map(lambda group: attend_head(group[0], group[1], group[2]), (query_all, key_all, value_all))
    attended = heads_out.transpose(1, 0, 2).reshape(SEQUENCE_TOKENS, HEADS * HDIM).astype(jnp.bfloat16)
    block_count = SEQUENCE_TOKENS // TOK_DEV
    input_blocks = ssm_input.reshape(block_count, TOK_DEV, STATE_SPACE_HEADS * SSM_HDIM)
    write_blocks = write_proj.reshape(block_count, TOK_DEV, STATE)
    read_blocks = read_proj.reshape(block_count, TOK_DEV, STATE)
    decay_blocks = log_decay.reshape(STATE_SPACE_HEADS, block_count, TOK_DEV).transpose(1, 0, 2)

    def advance(entering, block_parts):
        input_block, write_block, read_block, decay_block = block_parts
        cumulative, inner_part, local_state, total_decay = chain_pieces(input_block, write_block, read_block, decay_block)
        mixed_rows = chain_output(cumulative, inner_part, entering, read_block)
        leaving = total_decay[:, None, None] * entering + local_state
        return (leaving, mixed_rows)
    start_state = jnp.zeros((STATE_SPACE_HEADS, STATE, SSM_HDIM), jnp.float32)
    final_state, mixed_all = lax.scan(advance, start_state, (input_blocks, write_blocks, read_blocks, decay_blocks))
    ssm_mix = mixed_all.reshape(SEQUENCE_TOKENS, STATE_SPACE_HEADS * SSM_HDIM)
    update = jnp.dot(attended, attn_project, preferred_element_type=jnp.float32) + jnp.dot(ssm_mix, ssm_project, preferred_element_type=jnp.float32)
    block_out = (tokens.astype(jnp.float32) + update).astype(jnp.bfloat16)
    gauss = jnp.dot(block_out, gauss_project, preferred_element_type=jnp.float32).astype(jnp.bfloat16)
    one_hot = (tile_owner[:, None] == jnp.arange(OWNERS, dtype=jnp.int32)[None, :]).astype(jnp.int32)
    grouped = one_hot.reshape(SEQUENCE_TOKENS // SUB, SUB, OWNERS)
    slot_rank = lax.optimization_barrier(jnp.sum((jnp.cumsum(grouped, axis=1) - grouped) * grouped, axis=2)).reshape(SEQUENCE_TOKENS).astype(jnp.int32)
    token_positions = jnp.arange(SEQUENCE_TOKENS, dtype=jnp.int32)
    block_index = token_positions // TOK_DEV
    group_index = token_positions % TOK_DEV // SUB
    tile_rows = jnp.zeros((BLOCKS, OWNERS, OWNERS, CAP, GW), jnp.bfloat16)
    tile_rows = tile_rows.at[block_index, tile_owner, group_index, slot_rank].set(gauss)
    return (block_out, tile_rows)
```

```python
import math

import jax
import jax.numpy as jnp
from jax import lax
from jax.sharding import PartitionSpec as P

HDIM = 64


def chain_pieces(ssm_input, write_proj, read_proj, log_decay):
    row_count = write_proj.shape[0]
    head_count = log_decay.shape[0]
    head_width = ssm_input.shape[1] // head_count
    cumulative = jnp.cumsum(log_decay, axis=1)
    inputs_heads = ssm_input.reshape(row_count, head_count, head_width)
    later_rows = lax.broadcasted_iota(jnp.int32, (row_count, row_count), 0)
    earlier_cols = lax.broadcasted_iota(jnp.int32, (row_count, row_count), 1)
    log_gaps = cumulative[:, :, None] - cumulative[:, None, :]
    decays = jnp.exp(jnp.where((later_rows >= earlier_cols)[None], log_gaps, -jnp.inf))
    cross_terms = jnp.dot(read_proj, write_proj.T, preferred_element_type=jnp.float32)
    mixing = (decays * cross_terms[None]).astype(jnp.bfloat16)
    inner_part = jnp.einsum(
        "hts,shp->thp", mixing, inputs_heads, preferred_element_type=jnp.float32
    )
    tail_decay = jnp.exp(cumulative[:, -1:] - cumulative)
    tail_inputs = (inputs_heads.astype(jnp.float32) * tail_decay.T[:, :, None]).astype(jnp.bfloat16)
    local_state = jnp.einsum(
        "sn,shp->hnp", write_proj, tail_inputs, preferred_element_type=jnp.float32
    )
    total_decay = jnp.exp(cumulative[:, -1])
    return (cumulative, inner_part, local_state, total_decay)


def chain_output(cumulative, inner_part, entering, read_proj):
    entering_low = entering.astype(jnp.bfloat16)
    outer_part = jnp.einsum(
        "tn,hnp->thp", read_proj, entering_low, preferred_element_type=jnp.float32
    )
    mixture = inner_part + outer_part * jnp.exp(cumulative).T[:, :, None]
    scaled = mixture * lax.rsqrt(jnp.mean(mixture * mixture, axis=2, keepdims=True) + 1e-05)
    return scaled.reshape(scaled.shape[0], -1).astype(jnp.bfloat16)


def pass_states(local_state, total_decay):
    axis = "seq"
    devices = lax.axis_size(axis)
    mine = lax.axis_index(axis)

    def shifted(tree, distance):
        pairs = [(j, j + distance) for j in range(devices - distance)]
        return jax.tree.map(lambda part: lax.ppermute(part, axis, pairs), tree)

    decay, state = shifted((total_decay, local_state), 1)
    first = mine >= 1
    decay = jnp.where(first, decay, jnp.ones_like(decay))
    state = jnp.where(first, state, jnp.zeros_like(state))
    distance = 1
    while distance < devices:
        earlier_decay, earlier_state = shifted((decay, state), distance)
        reached = mine >= distance
        new_decay = earlier_decay * decay
        new_state = decay[:, None, None] * earlier_state + state
        decay = jnp.where(reached, new_decay, decay)
        state = jnp.where(reached, new_state, state)
        distance *= 2
    return state


def fold_keys(query_heads, key_rows, values):
    row_count, head_count, head_width = query_heads.shape
    scale = 1.0 / math.sqrt(head_width)
    initial = (
        jnp.full((head_count, row_count), -jnp.inf, jnp.float32),
        jnp.zeros((head_count, row_count), jnp.float32),
        jnp.zeros((head_count, row_count, head_width), jnp.float32),
    )
    key_piece = lax.all_gather(key_rows, "seq", axis=0, tiled=True)
    value_piece = lax.all_gather(values, "seq", axis=0, tiled=True)
    piece_rows = key_piece.shape[0]
    block_rows = math.gcd(piece_rows, 1024)

    def one_step(block_index, carry_state):
        run_max, run_sum, accumulated = carry_state
        key_block = lax.dynamic_slice_in_dim(
            key_piece, block_index * block_rows, block_rows, 0
        ).reshape(block_rows, head_count, head_width)
        value_block = lax.dynamic_slice_in_dim(
            value_piece, block_index * block_rows, block_rows, 0
        ).reshape(block_rows, head_count, head_width)
        scores = (
            jnp.einsum("qhd,khd->hqk", query_heads, key_block, preferred_element_type=jnp.float32)
            * scale
        )
        new_max = jnp.maximum(run_max, jnp.max(scores, axis=2))
        shrink = jnp.exp(run_max - new_max)
        raised = jnp.exp(scores - new_max[:, :, None])
        run_sum = run_sum * shrink + jnp.sum(raised, axis=2)
        accumulated = accumulated * shrink[:, :, None] + jnp.einsum(
            "hqk,khd->hqd",
            raised.astype(jnp.bfloat16),
            value_block,
            preferred_element_type=jnp.float32,
        )
        return (new_max, run_sum, accumulated)

    run_max, run_sum, accumulated = lax.fori_loop(0, piece_rows // block_rows, one_step, initial)
    attended = accumulated / run_sum[:, :, None]
    return (
        attended.transpose(1, 0, 2).reshape(row_count, head_count * head_width).astype(jnp.bfloat16)
    )


def slot_rank(owners_here, owner_count, group_rows):
    row_count = owners_here.shape[0]
    one_hot = (owners_here[:, None] == jnp.arange(owner_count, dtype=jnp.int32)[None, :]).astype(
        jnp.bfloat16
    )
    later_rows = lax.broadcasted_iota(jnp.int32, (row_count, row_count), 0)
    earlier_cols = lax.broadcasted_iota(jnp.int32, (row_count, row_count), 1)
    before = (
        (earlier_cols < later_rows) & (later_rows // group_rows == earlier_cols // group_rows)
    ).astype(jnp.bfloat16)
    counted = jnp.dot(before, one_hot, preferred_element_type=jnp.float32)
    return jnp.sum(counted * one_hot.astype(jnp.float32), axis=1)


def per_device(
    tokens,
    queries,
    key_rows,
    values,
    ssm_input,
    write_proj,
    read_proj,
    log_decay,
    attn_project,
    ssm_project,
    gauss_project,
    tile_owner,
):
    row_count = queries.shape[0]
    head_count = queries.shape[1] // HDIM
    query_heads = queries.reshape(row_count, head_count, HDIM)
    attended = fold_keys(query_heads, key_rows, values)
    cumulative, inner_part, local_state, total_decay = chain_pieces(
        ssm_input, write_proj, read_proj, log_decay
    )
    entering = pass_states(local_state, total_decay)
    ssm_mix = chain_output(cumulative, inner_part, entering, read_proj)
    owner_count = lax.axis_size("head")
    own_index = lax.axis_index("head")
    sub_rows = row_count // owner_count
    capacity = sub_rows // 2
    width_out = gauss_project.shape[1]
    slot_count = owner_count * capacity
    slot_ids = jnp.arange(slot_count, dtype=jnp.float32)
    update = lax.psum_scatter(
        (
            jnp.dot(attended, attn_project, preferred_element_type=jnp.float32)
            + jnp.dot(ssm_mix, ssm_project, preferred_element_type=jnp.float32)
        ).astype(jnp.bfloat16),
        "head",
        scatter_dimension=0,
        tiled=True,
    ).astype(jnp.float32)
    own_tokens = lax.dynamic_slice_in_dim(tokens, own_index * sub_rows, sub_rows, 0)
    block_out = (own_tokens.astype(jnp.float32) + update).astype(jnp.bfloat16)
    gaussians = jnp.dot(block_out, gauss_project, preferred_element_type=jnp.float32).astype(
        jnp.bfloat16
    )
    owners_here = lax.dynamic_slice_in_dim(tile_owner, own_index * sub_rows, sub_rows, 0)
    slot_value = owners_here.astype(jnp.float32) * capacity + slot_rank(
        owners_here, owner_count, sub_rows
    )
    selector = (slot_ids[:, None] == slot_value[None, :]).astype(jnp.bfloat16)
    packed = jnp.dot(selector, gaussians, preferred_element_type=jnp.float32).astype(jnp.bfloat16)
    packed = packed.reshape(owner_count, capacity, width_out)
    received = lax.all_to_all(packed, "head", split_axis=0, concat_axis=0, tiled=True)
    tile_rows = received.reshape(1, 1, owner_count, capacity, width_out)
    return (block_out, tile_rows)


def solution(mesh):
    in_specs = (
        P("seq", None),
        P("seq", "head"),
        P("seq", "head"),
        P("seq", "head"),
        P("seq", "head"),
        P("seq", None),
        P("seq", None),
        P("head", "seq"),
        P("head", None),
        P("head", None),
        P(),
        P("seq"),
    )
    out_specs = (P(("seq", "head"), None), P("seq", "head", None, None, None))
    return jax.shard_map(
        per_device, mesh=mesh, in_specs=in_specs, out_specs=out_specs, check_vma=False
    )
```

```python
import math

import jax
import jax.numpy as jnp
from jax import lax
from jax.sharding import Mesh, PartitionSpec as P

HDIM = 64


def chain_pieces(ssm_input, write_proj, read_proj, log_decay):
    row_count = write_proj.shape[0]
    head_count = log_decay.shape[0]
    head_width = ssm_input.shape[1] // head_count
    cumulative = jnp.cumsum(log_decay, axis=1)
    inputs_heads = ssm_input.reshape(row_count, head_count, head_width)
    later_rows = lax.broadcasted_iota(jnp.int32, (row_count, row_count), 0)
    earlier_cols = lax.broadcasted_iota(jnp.int32, (row_count, row_count), 1)
    log_gaps = cumulative[:, :, None] - cumulative[:, None, :]
    decays = jnp.exp(jnp.where((later_rows >= earlier_cols)[None], log_gaps, -jnp.inf))
    cross_terms = jnp.dot(read_proj, write_proj.T, preferred_element_type=jnp.float32)
    mixing = (decays * cross_terms[None]).astype(jnp.bfloat16)
    inner_part = jnp.einsum(
        "hts,shp->thp", mixing, inputs_heads, preferred_element_type=jnp.float32
    )
    tail_decay = jnp.exp(cumulative[:, -1:] - cumulative)
    tail_inputs = (inputs_heads.astype(jnp.float32) * tail_decay.T[:, :, None]).astype(jnp.bfloat16)
    local_state = jnp.einsum(
        "sn,shp->hnp", write_proj, tail_inputs, preferred_element_type=jnp.float32
    )
    total_decay = jnp.exp(cumulative[:, -1])
    return (cumulative, inner_part, local_state, total_decay)


def chain_output(cumulative, inner_part, entering, read_proj):
    entering_low = entering.astype(jnp.bfloat16)
    outer_part = jnp.einsum(
        "tn,hnp->thp", read_proj, entering_low, preferred_element_type=jnp.float32
    )
    mixture = inner_part + outer_part * jnp.exp(cumulative).T[:, :, None]
    scaled = mixture * lax.rsqrt(jnp.mean(mixture * mixture, axis=2, keepdims=True) + 1e-05)
    return scaled.reshape(scaled.shape[0], -1).astype(jnp.bfloat16)


def pass_states(local_state, total_decay):
    axis = ("sa", "sb")
    devices = lax.axis_size(axis)
    mine = lax.axis_index(axis)

    def shifted(tree, distance):
        pairs = [(j, j + distance) for j in range(devices - distance)]
        return jax.tree.map(lambda part: lax.ppermute(part, axis, pairs), tree)

    decay, state = shifted((total_decay, local_state), 1)
    first = mine >= 1
    decay = jnp.where(first, decay, jnp.ones_like(decay))
    state = jnp.where(first, state, jnp.zeros_like(state))
    distance = 1
    while distance < devices:
        earlier_decay, earlier_state = shifted((decay, state), distance)
        reached = mine >= distance
        new_decay = earlier_decay * decay
        new_state = decay[:, None, None] * earlier_state + state
        decay = jnp.where(reached, new_decay, decay)
        state = jnp.where(reached, new_state, state)
        distance *= 2
    return state


def fold_keys(query_heads, key_rows, values):
    row_count, head_count, head_width = query_heads.shape
    scale = 1.0 / math.sqrt(head_width)
    initial = (
        jnp.full((head_count, row_count), -jnp.inf, jnp.float32),
        jnp.zeros((head_count, row_count), jnp.float32),
        jnp.zeros((head_count, row_count, head_width), jnp.float32),
    )
    key_piece = lax.all_gather(key_rows, "sa", axis=0, tiled=True)
    value_piece = lax.all_gather(values, "sa", axis=0, tiled=True)
    piece_rows = key_piece.shape[0]
    block_rows = math.gcd(piece_rows, 1024)

    def one_step(block_index, carry_state):
        run_max, run_sum, accumulated = carry_state
        key_block = lax.dynamic_slice_in_dim(
            key_piece, block_index * block_rows, block_rows, 0
        ).reshape(block_rows, head_count, head_width)
        value_block = lax.dynamic_slice_in_dim(
            value_piece, block_index * block_rows, block_rows, 0
        ).reshape(block_rows, head_count, head_width)
        scores = (
            jnp.einsum("qhd,khd->hqk", query_heads, key_block, preferred_element_type=jnp.float32)
            * scale
        )
        new_max = jnp.maximum(run_max, jnp.max(scores, axis=2))
        shrink = jnp.exp(run_max - new_max)
        raised = jnp.exp(scores - new_max[:, :, None])
        run_sum = run_sum * shrink + jnp.sum(raised, axis=2)
        accumulated = accumulated * shrink[:, :, None] + jnp.einsum(
            "hqk,khd->hqd",
            raised.astype(jnp.bfloat16),
            value_block,
            preferred_element_type=jnp.float32,
        )
        return (new_max, run_sum, accumulated)

    run_max, run_sum, accumulated = lax.fori_loop(0, piece_rows // block_rows, one_step, initial)
    attended = accumulated / run_sum[:, :, None]
    return (
        attended.transpose(1, 0, 2).reshape(row_count, head_count * head_width).astype(jnp.bfloat16)
    )


def slot_rank(owners_here, owner_count, group_rows):
    row_count = owners_here.shape[0]
    one_hot = (owners_here[:, None] == jnp.arange(owner_count, dtype=jnp.int32)[None, :]).astype(
        jnp.bfloat16
    )
    later_rows = lax.broadcasted_iota(jnp.int32, (row_count, row_count), 0)
    earlier_cols = lax.broadcasted_iota(jnp.int32, (row_count, row_count), 1)
    before = (
        (earlier_cols < later_rows) & (later_rows // group_rows == earlier_cols // group_rows)
    ).astype(jnp.bfloat16)
    counted = jnp.dot(before, one_hot, preferred_element_type=jnp.float32)
    return jnp.sum(counted * one_hot.astype(jnp.float32), axis=1)


def per_device(
    tokens,
    queries,
    key_rows,
    values,
    ssm_input,
    write_proj,
    read_proj,
    log_decay,
    attn_project,
    ssm_project,
    gauss_project,
    tile_owner,
):
    row_count = queries.shape[0]
    head_count = queries.shape[1] // HDIM

    def spread(part):
        split = part.reshape(row_count, head_count, HDIM)
        return lax.all_to_all(split, "sb", split_axis=1, concat_axis=0, tiled=True)

    query_heads = spread(queries)
    group_keys = spread(key_rows).reshape(-1, HDIM)
    group_values = spread(values).reshape(-1, HDIM)
    attended_one = fold_keys(query_heads, group_keys, group_values)
    attended = lax.all_to_all(
        attended_one.reshape(-1, 1, HDIM), "sb", split_axis=0, concat_axis=1, tiled=True
    ).reshape(row_count, head_count * HDIM)
    cumulative, inner_part, local_state, total_decay = chain_pieces(
        ssm_input, write_proj, read_proj, log_decay
    )
    entering = pass_states(local_state, total_decay)
    ssm_mix = chain_output(cumulative, inner_part, entering, read_proj)
    owner_count = lax.axis_size("head")
    own_index = lax.axis_index("head")
    sub_rows = row_count // owner_count
    capacity = sub_rows // 2
    width_out = gauss_project.shape[1]
    slot_count = owner_count * capacity
    slot_ids = jnp.arange(slot_count, dtype=jnp.float32)
    update = lax.psum_scatter(
        (
            jnp.dot(attended, attn_project, preferred_element_type=jnp.float32)
            + jnp.dot(ssm_mix, ssm_project, preferred_element_type=jnp.float32)
        ).astype(jnp.bfloat16),
        "head",
        scatter_dimension=0,
        tiled=True,
    ).astype(jnp.float32)
    own_tokens = lax.dynamic_slice_in_dim(tokens, own_index * sub_rows, sub_rows, 0)
    block_out = (own_tokens.astype(jnp.float32) + update).astype(jnp.bfloat16)
    gaussians = jnp.dot(block_out, gauss_project, preferred_element_type=jnp.float32).astype(
        jnp.bfloat16
    )
    owners_here = lax.dynamic_slice_in_dim(tile_owner, own_index * sub_rows, sub_rows, 0)
    slot_value = owners_here.astype(jnp.float32) * capacity + slot_rank(
        owners_here, owner_count, sub_rows
    )
    selector = (slot_ids[:, None] == slot_value[None, :]).astype(jnp.bfloat16)
    packed = jnp.dot(selector, gaussians, preferred_element_type=jnp.float32).astype(jnp.bfloat16)
    packed = packed.reshape(owner_count, capacity, width_out)
    received = lax.all_to_all(packed, "head", split_axis=0, concat_axis=0, tiled=True)
    tile_rows = received.reshape(1, 1, owner_count, capacity, width_out)
    return (block_out, tile_rows)


def solution(mesh):
    seq_count = mesh.shape["seq"]
    inner = math.gcd(seq_count, mesh.shape["head"])
    split_mesh = Mesh(
        mesh.devices.reshape(seq_count // inner, inner, mesh.shape["head"]), ("sa", "sb", "head")
    )
    seq = ("sa", "sb")
    in_specs = (
        P(seq, None),
        P(seq, "head"),
        P(seq, "head"),
        P(seq, "head"),
        P(seq, "head"),
        P(seq, None),
        P(seq, None),
        P("head", seq),
        P("head", None),
        P("head", None),
        P(),
        P(seq),
    )
    out_specs = (P(("sa", "sb", "head"), None), P(seq, "head", None, None, None))
    return jax.shard_map(
        per_device, mesh=split_mesh, in_specs=in_specs, out_specs=out_specs, check_vma=False
    )
```

```python
import math

import jax
import jax.numpy as jnp
from jax import lax
from jax.sharding import Mesh, PartitionSpec as P

HDIM = 64


def chain_pieces(ssm_input, write_proj, read_proj, log_decay):
    row_count = write_proj.shape[0]
    head_count = log_decay.shape[0]
    head_width = ssm_input.shape[1] // head_count
    cumulative = jnp.cumsum(log_decay, axis=1)
    inputs_heads = ssm_input.reshape(row_count, head_count, head_width)
    later_rows = lax.broadcasted_iota(jnp.int32, (row_count, row_count), 0)
    earlier_cols = lax.broadcasted_iota(jnp.int32, (row_count, row_count), 1)
    log_gaps = cumulative[:, :, None] - cumulative[:, None, :]
    decays = jnp.exp(jnp.where((later_rows >= earlier_cols)[None], log_gaps, -jnp.inf))
    cross_terms = jnp.dot(read_proj, write_proj.T, preferred_element_type=jnp.float32)
    mixing = (decays * cross_terms[None]).astype(jnp.bfloat16)
    inner_part = jnp.einsum(
        "hts,shp->thp", mixing, inputs_heads, preferred_element_type=jnp.float32
    )
    tail_decay = jnp.exp(cumulative[:, -1:] - cumulative)
    tail_inputs = (inputs_heads.astype(jnp.float32) * tail_decay.T[:, :, None]).astype(jnp.bfloat16)
    local_state = jnp.einsum(
        "sn,shp->hnp", write_proj, tail_inputs, preferred_element_type=jnp.float32
    )
    total_decay = jnp.exp(cumulative[:, -1])
    return (cumulative, inner_part, local_state, total_decay)


def chain_output(cumulative, inner_part, entering, read_proj):
    entering_low = entering.astype(jnp.bfloat16)
    outer_part = jnp.einsum(
        "tn,hnp->thp", read_proj, entering_low, preferred_element_type=jnp.float32
    )
    mixture = inner_part + outer_part * jnp.exp(cumulative).T[:, :, None]
    scaled = mixture * lax.rsqrt(jnp.mean(mixture * mixture, axis=2, keepdims=True) + 1e-05)
    return scaled.reshape(scaled.shape[0], -1).astype(jnp.bfloat16)


def pass_states(local_state, total_decay):
    axis = ("sa", "sb")
    devices = lax.axis_size(axis)
    mine = lax.axis_index(axis)

    def shifted(tree, distance):
        pairs = [(j, j + distance) for j in range(devices - distance)]
        return jax.tree.map(lambda part: lax.ppermute(part, axis, pairs), tree)

    decay, state = shifted((total_decay, local_state), 1)
    first = mine >= 1
    decay = jnp.where(first, decay, jnp.ones_like(decay))
    state = jnp.where(first, state, jnp.zeros_like(state))
    distance = 1
    while distance < devices:
        earlier_decay, earlier_state = shifted((decay, state), distance)
        reached = mine >= distance
        new_decay = earlier_decay * decay
        new_state = decay[:, None, None] * earlier_state + state
        decay = jnp.where(reached, new_decay, decay)
        state = jnp.where(reached, new_state, state)
        distance *= 2
    return state


def fold_keys(query_heads, key_rows, values):
    row_count, head_count, head_width = query_heads.shape
    scale = 1.0 / math.sqrt(head_width)
    initial = (
        jnp.full((head_count, row_count), -jnp.inf, jnp.float32),
        jnp.zeros((head_count, row_count), jnp.float32),
        jnp.zeros((head_count, row_count, head_width), jnp.float32),
    )
    key_piece = key_rows
    value_piece = values
    piece_rows = key_piece.shape[0]
    block_rows = math.gcd(piece_rows, 1024)

    def one_step(block_index, carry_state):
        run_max, run_sum, accumulated = carry_state
        key_block = lax.dynamic_slice_in_dim(
            key_piece, block_index * block_rows, block_rows, 0
        ).reshape(block_rows, head_count, head_width)
        value_block = lax.dynamic_slice_in_dim(
            value_piece, block_index * block_rows, block_rows, 0
        ).reshape(block_rows, head_count, head_width)
        scores = (
            jnp.einsum("qhd,khd->hqk", query_heads, key_block, preferred_element_type=jnp.float32)
            * scale
        )
        new_max = jnp.maximum(run_max, jnp.max(scores, axis=2))
        shrink = jnp.exp(run_max - new_max)
        raised = jnp.exp(scores - new_max[:, :, None])
        run_sum = run_sum * shrink + jnp.sum(raised, axis=2)
        accumulated = accumulated * shrink[:, :, None] + jnp.einsum(
            "hqk,khd->hqd",
            raised.astype(jnp.bfloat16),
            value_block,
            preferred_element_type=jnp.float32,
        )
        return (new_max, run_sum, accumulated)

    run_max, run_sum, accumulated = lax.fori_loop(0, piece_rows // block_rows, one_step, initial)
    attended = accumulated / run_sum[:, :, None]
    return (
        attended.transpose(1, 0, 2).reshape(row_count, head_count * head_width).astype(jnp.bfloat16)
    )


def slot_rank(owners_here, owner_count, group_rows):
    row_count = owners_here.shape[0]
    one_hot = (owners_here[:, None] == jnp.arange(owner_count, dtype=jnp.int32)[None, :]).astype(
        jnp.bfloat16
    )
    later_rows = lax.broadcasted_iota(jnp.int32, (row_count, row_count), 0)
    earlier_cols = lax.broadcasted_iota(jnp.int32, (row_count, row_count), 1)
    before = (
        (earlier_cols < later_rows) & (later_rows // group_rows == earlier_cols // group_rows)
    ).astype(jnp.bfloat16)
    counted = jnp.dot(before, one_hot, preferred_element_type=jnp.float32)
    return jnp.sum(counted * one_hot.astype(jnp.float32), axis=1)


def per_device(
    tokens,
    queries,
    key_rows,
    values,
    ssm_input,
    write_proj,
    read_proj,
    log_decay,
    attn_project,
    ssm_project,
    gauss_project,
    tile_owner,
):
    row_count = queries.shape[0]
    head_count = queries.shape[1] // HDIM

    stacked = jnp.stack([queries, key_rows, values]).reshape(3, row_count, head_count, HDIM)
    spread = lax.all_to_all(stacked, "sb", split_axis=2, concat_axis=1, tiled=True)
    query_heads = spread[0]
    group_rows = spread.shape[1]
    peers = lax.axis_size("sa")
    pair = spread[1:].reshape(2, group_rows, HDIM)
    gathered = lax.all_to_all(
        jnp.broadcast_to(pair[None], (peers, 2, group_rows, HDIM)),
        "sa",
        split_axis=0,
        concat_axis=0,
        tiled=True,
    )
    group_keys = gathered[:, 0].reshape(peers * group_rows, HDIM)
    group_values = gathered[:, 1].reshape(peers * group_rows, HDIM)
    attended_one = fold_keys(query_heads, group_keys, group_values)
    attended = lax.all_to_all(
        attended_one.reshape(-1, 1, HDIM), "sb", split_axis=0, concat_axis=1, tiled=True
    ).reshape(row_count, head_count * HDIM)
    cumulative, inner_part, local_state, total_decay = chain_pieces(
        ssm_input, write_proj, read_proj, log_decay
    )
    entering = pass_states(local_state, total_decay)
    ssm_mix = chain_output(cumulative, inner_part, entering, read_proj)
    owner_count = lax.axis_size("head")
    own_index = lax.axis_index("head")
    sub_rows = row_count // owner_count
    capacity = sub_rows // 2
    width_out = gauss_project.shape[1]
    slot_count = owner_count * capacity
    slot_ids = jnp.arange(slot_count, dtype=jnp.float32)
    update = lax.psum_scatter(
        (
            jnp.dot(attended, attn_project, preferred_element_type=jnp.float32)
            + jnp.dot(ssm_mix, ssm_project, preferred_element_type=jnp.float32)
        ).astype(jnp.bfloat16),
        "head",
        scatter_dimension=0,
        tiled=True,
    ).astype(jnp.float32)
    own_tokens = lax.dynamic_slice_in_dim(tokens, own_index * sub_rows, sub_rows, 0)
    block_out = (own_tokens.astype(jnp.float32) + update).astype(jnp.bfloat16)
    gaussians = jnp.dot(block_out, gauss_project, preferred_element_type=jnp.float32).astype(
        jnp.bfloat16
    )
    owners_here = lax.dynamic_slice_in_dim(tile_owner, own_index * sub_rows, sub_rows, 0)
    slot_value = owners_here.astype(jnp.float32) * capacity + slot_rank(
        owners_here, owner_count, sub_rows
    )
    selector = (slot_ids[:, None] == slot_value[None, :]).astype(jnp.bfloat16)
    packed = jnp.dot(selector, gaussians, preferred_element_type=jnp.float32).astype(jnp.bfloat16)
    packed = packed.reshape(owner_count, capacity, width_out)
    received = lax.all_to_all(packed, "head", split_axis=0, concat_axis=0, tiled=True)
    tile_rows = received.reshape(1, 1, owner_count, capacity, width_out)
    return (block_out, tile_rows)


def solution(mesh):
    seq_count = mesh.shape["seq"]
    inner = math.gcd(seq_count, mesh.shape["head"])
    split_mesh = Mesh(
        mesh.devices.reshape(seq_count // inner, inner, mesh.shape["head"]), ("sa", "sb", "head")
    )
    seq = ("sa", "sb")
    in_specs = (
        P(seq, None),
        P(seq, "head"),
        P(seq, "head"),
        P(seq, "head"),
        P(seq, "head"),
        P(seq, None),
        P(seq, None),
        P("head", seq),
        P("head", None),
        P("head", None),
        P(),
        P(seq),
    )
    out_specs = (P(("sa", "sb", "head"), None), P(seq, "head", None, None, None))
    return jax.shard_map(
        per_device, mesh=split_mesh, in_specs=in_specs, out_specs=out_specs, check_vma=False
    )
```

```python
import math

import jax
import jax.numpy as jnp
from jax import lax
from jax.sharding import Mesh, PartitionSpec as P

HDIM = 64


def chain_pieces(ssm_input, write_proj, read_proj, log_decay):
    row_count = write_proj.shape[0]
    head_count = log_decay.shape[0]
    head_width = ssm_input.shape[1] // head_count
    cumulative = jnp.cumsum(log_decay, axis=1)
    inputs_heads = ssm_input.reshape(row_count, head_count, head_width)
    later_rows = lax.broadcasted_iota(jnp.int32, (row_count, row_count), 0)
    earlier_cols = lax.broadcasted_iota(jnp.int32, (row_count, row_count), 1)
    log_gaps = cumulative[:, :, None] - cumulative[:, None, :]
    decays = jnp.exp(jnp.where((later_rows >= earlier_cols)[None], log_gaps, -jnp.inf))
    cross_terms = jnp.dot(read_proj, write_proj.T, preferred_element_type=jnp.float32)
    mixing = (decays * cross_terms[None]).astype(jnp.bfloat16)
    inner_part = jnp.einsum(
        "hts,shp->thp", mixing, inputs_heads, preferred_element_type=jnp.float32
    )
    tail_decay = jnp.exp(cumulative[:, -1:] - cumulative)
    tail_inputs = (inputs_heads.astype(jnp.float32) * tail_decay.T[:, :, None]).astype(jnp.bfloat16)
    local_state = jnp.einsum(
        "sn,shp->hnp", write_proj, tail_inputs, preferred_element_type=jnp.float32
    )
    total_decay = jnp.exp(cumulative[:, -1])
    return (cumulative, inner_part, local_state, total_decay)


def chain_output(cumulative, inner_part, entering, read_proj):
    entering_low = entering.astype(jnp.bfloat16)
    outer_part = jnp.einsum(
        "tn,hnp->thp", read_proj, entering_low, preferred_element_type=jnp.float32
    )
    mixture = inner_part + outer_part * jnp.exp(cumulative).T[:, :, None]
    scaled = mixture * lax.rsqrt(jnp.mean(mixture * mixture, axis=2, keepdims=True) + 1e-05)
    return scaled.reshape(scaled.shape[0], -1).astype(jnp.bfloat16)


def pass_states(local_state, total_decay):
    axis = ("sa", "sb")
    devices = lax.axis_size(axis)
    mine = lax.axis_index(axis)

    def shifted(tree, distance):
        pairs = [(j, j + distance) for j in range(devices - distance)]
        return jax.tree.map(lambda part: lax.ppermute(part, axis, pairs), tree)

    decay, state = shifted((total_decay, local_state), 1)
    first = mine >= 1
    decay = jnp.where(first, decay, jnp.ones_like(decay))
    state = jnp.where(first, state, jnp.zeros_like(state))
    distance = 1
    while distance < devices:
        earlier_decay, earlier_state = shifted((decay, state), distance)
        reached = mine >= distance
        new_decay = earlier_decay * decay
        new_state = decay[:, None, None] * earlier_state + state
        decay = jnp.where(reached, new_decay, decay)
        state = jnp.where(reached, new_state, state)
        distance *= 2
    return state


def fold_keys(query_heads, key_rows, values):
    row_count, head_count, head_width = query_heads.shape
    scale = 1.0 / math.sqrt(head_width)
    initial = (
        jnp.full((head_count, row_count), -jnp.inf, jnp.float32),
        jnp.zeros((head_count, row_count), jnp.float32),
        jnp.zeros((head_count, row_count, head_width), jnp.float32),
    )
    key_piece = key_rows
    value_piece = values
    piece_rows = key_piece.shape[0]
    block_rows = math.gcd(piece_rows, 1024)

    def one_step(block_index, carry_state):
        run_max, run_sum, accumulated = carry_state
        key_block = lax.dynamic_slice_in_dim(
            key_piece, block_index * block_rows, block_rows, 0
        ).reshape(block_rows, head_count, head_width)
        value_block = lax.dynamic_slice_in_dim(
            value_piece, block_index * block_rows, block_rows, 0
        ).reshape(block_rows, head_count, head_width)
        scores = (
            jnp.einsum("qhd,khd->hqk", query_heads, key_block, preferred_element_type=jnp.float32)
            * scale
        )
        new_max = jnp.maximum(run_max, jnp.max(scores, axis=2))
        shrink = jnp.exp(run_max - new_max)
        raised = jnp.exp(scores - new_max[:, :, None])
        run_sum = run_sum * shrink + jnp.sum(raised, axis=2)
        accumulated = accumulated * shrink[:, :, None] + jnp.einsum(
            "hqk,khd->hqd",
            raised.astype(jnp.bfloat16),
            value_block,
            preferred_element_type=jnp.float32,
        )
        return (new_max, run_sum, accumulated)

    run_max, run_sum, accumulated = lax.fori_loop(0, piece_rows // block_rows, one_step, initial)
    attended = accumulated / run_sum[:, :, None]
    return (
        attended.transpose(1, 0, 2).reshape(row_count, head_count * head_width).astype(jnp.bfloat16)
    )


def slot_rank(owners_here, owner_count, group_rows):
    row_count = owners_here.shape[0]
    one_hot = (owners_here[:, None] == jnp.arange(owner_count, dtype=jnp.int32)[None, :]).astype(
        jnp.bfloat16
    )
    later_rows = lax.broadcasted_iota(jnp.int32, (row_count, row_count), 0)
    earlier_cols = lax.broadcasted_iota(jnp.int32, (row_count, row_count), 1)
    before = (
        (earlier_cols < later_rows) & (later_rows // group_rows == earlier_cols // group_rows)
    ).astype(jnp.bfloat16)
    counted = jnp.dot(before, one_hot, preferred_element_type=jnp.float32)
    return jnp.sum(counted * one_hot.astype(jnp.float32), axis=1)


def per_device(
    tokens,
    queries,
    key_rows,
    values,
    ssm_input,
    write_proj,
    read_proj,
    log_decay,
    attn_project,
    ssm_project,
    gauss_project,
    tile_owner,
):
    row_count = queries.shape[0]
    head_count = queries.shape[1] // HDIM

    def spread(part):
        split = part.reshape(row_count, head_count, HDIM)
        return lax.all_to_all(split, "sb", split_axis=1, concat_axis=0, tiled=True)

    query_heads = spread(queries)
    pair = jnp.stack([spread(key_rows), spread(values)]).reshape(2, -1, HDIM)
    gathered = lax.all_gather(pair, "sa", axis=1, tiled=True)
    group_keys = gathered[0]
    group_values = gathered[1]
    attended_one = fold_keys(query_heads, group_keys, group_values)
    attended = lax.all_to_all(
        attended_one.reshape(-1, 1, HDIM), "sb", split_axis=0, concat_axis=1, tiled=True
    ).reshape(row_count, head_count * HDIM)
    cumulative, inner_part, local_state, total_decay = chain_pieces(
        ssm_input, write_proj, read_proj, log_decay
    )
    entering = pass_states(local_state, total_decay)
    ssm_mix = chain_output(cumulative, inner_part, entering, read_proj)
    owner_count = lax.axis_size("head")
    own_index = lax.axis_index("head")
    sub_rows = row_count // owner_count
    capacity = sub_rows // 2
    width_out = gauss_project.shape[1]
    slot_count = owner_count * capacity
    slot_ids = jnp.arange(slot_count, dtype=jnp.float32)
    update = lax.psum_scatter(
        (
            jnp.dot(attended, attn_project, preferred_element_type=jnp.float32)
            + jnp.dot(ssm_mix, ssm_project, preferred_element_type=jnp.float32)
        ).astype(jnp.bfloat16),
        "head",
        scatter_dimension=0,
        tiled=True,
    ).astype(jnp.float32)
    own_tokens = lax.dynamic_slice_in_dim(tokens, own_index * sub_rows, sub_rows, 0)
    block_out = (own_tokens.astype(jnp.float32) + update).astype(jnp.bfloat16)
    gaussians = jnp.dot(block_out, gauss_project, preferred_element_type=jnp.float32).astype(
        jnp.bfloat16
    )
    owners_here = lax.dynamic_slice_in_dim(tile_owner, own_index * sub_rows, sub_rows, 0)
    slot_value = owners_here.astype(jnp.float32) * capacity + slot_rank(
        owners_here, owner_count, sub_rows
    )
    selector = (slot_ids[:, None] == slot_value[None, :]).astype(jnp.bfloat16)
    packed = jnp.dot(selector, gaussians, preferred_element_type=jnp.float32).astype(jnp.bfloat16)
    packed = packed.reshape(owner_count, capacity, width_out)
    received = lax.all_to_all(packed, "head", split_axis=0, concat_axis=0, tiled=True)
    tile_rows = received.reshape(1, 1, owner_count, capacity, width_out)
    return (block_out, tile_rows)


def solution(mesh):
    seq_count = mesh.shape["seq"]
    inner = math.gcd(seq_count, mesh.shape["head"])
    split_mesh = Mesh(
        mesh.devices.reshape(seq_count // inner, inner, mesh.shape["head"]), ("sa", "sb", "head")
    )
    seq = ("sa", "sb")
    in_specs = (
        P(seq, None),
        P(seq, "head"),
        P(seq, "head"),
        P(seq, "head"),
        P(seq, "head"),
        P(seq, None),
        P(seq, None),
        P("head", seq),
        P("head", None),
        P("head", None),
        P(),
        P(seq),
    )
    out_specs = (P(("sa", "sb", "head"), None), P(seq, "head", None, None, None))
    return jax.shard_map(
        per_device, mesh=split_mesh, in_specs=in_specs, out_specs=out_specs, check_vma=False
    )
```

```python
import math

import jax
import jax.numpy as jnp
from jax import lax
from jax.sharding import Mesh, PartitionSpec as P

HDIM = 64


def chain_pieces(ssm_input, write_proj, read_proj, log_decay):
    row_count = write_proj.shape[0]
    head_count = log_decay.shape[0]
    head_width = ssm_input.shape[1] // head_count
    cumulative = jnp.cumsum(log_decay, axis=1)
    inputs_heads = ssm_input.reshape(row_count, head_count, head_width)
    later_rows = lax.broadcasted_iota(jnp.int32, (row_count, row_count), 0)
    earlier_cols = lax.broadcasted_iota(jnp.int32, (row_count, row_count), 1)
    log_gaps = cumulative[:, :, None] - cumulative[:, None, :]
    decays = jnp.exp(jnp.where((later_rows >= earlier_cols)[None], log_gaps, -jnp.inf))
    cross_terms = jnp.dot(read_proj, write_proj.T, preferred_element_type=jnp.float32)
    mixing = (decays * cross_terms[None]).astype(jnp.bfloat16)
    inner_part = jnp.einsum(
        "hts,shp->thp", mixing, inputs_heads, preferred_element_type=jnp.float32
    )
    tail_decay = jnp.exp(cumulative[:, -1:] - cumulative)
    tail_inputs = (inputs_heads.astype(jnp.float32) * tail_decay.T[:, :, None]).astype(jnp.bfloat16)
    local_state = jnp.einsum(
        "sn,shp->hnp", write_proj, tail_inputs, preferred_element_type=jnp.float32
    )
    total_decay = jnp.exp(cumulative[:, -1])
    return (cumulative, inner_part, local_state, total_decay)


def chain_output(cumulative, inner_part, entering, read_proj):
    entering_low = entering.astype(jnp.bfloat16)
    outer_part = jnp.einsum(
        "tn,hnp->thp", read_proj, entering_low, preferred_element_type=jnp.float32
    )
    mixture = inner_part + outer_part * jnp.exp(cumulative).T[:, :, None]
    scaled = mixture * lax.rsqrt(jnp.mean(mixture * mixture, axis=2, keepdims=True) + 1e-05)
    return scaled.reshape(scaled.shape[0], -1).astype(jnp.bfloat16)


def pass_states(local_state, total_decay):
    axis = ("sb", "sa")
    devices = lax.axis_size(axis)
    mine = lax.axis_index(axis)

    def shifted(tree, distance):
        pairs = [(j, j + distance) for j in range(devices - distance)]
        return jax.tree.map(lambda part: lax.ppermute(part, axis, pairs), tree)

    decay, state = shifted((total_decay, local_state), 1)
    first = mine >= 1
    decay = jnp.where(first, decay, jnp.ones_like(decay))
    state = jnp.where(first, state, jnp.zeros_like(state))
    distance = 1
    while distance < devices:
        earlier_decay, earlier_state = shifted((decay, state), distance)
        reached = mine >= distance
        new_decay = earlier_decay * decay
        new_state = decay[:, None, None] * earlier_state + state
        decay = jnp.where(reached, new_decay, decay)
        state = jnp.where(reached, new_state, state)
        distance *= 2
    return state


def fold_keys(query_heads, key_rows, values):
    row_count, head_count, head_width = query_heads.shape
    scale = 1.0 / math.sqrt(head_width)
    initial = (
        jnp.full((head_count, row_count), -jnp.inf, jnp.float32),
        jnp.zeros((head_count, row_count), jnp.float32),
        jnp.zeros((head_count, row_count, head_width), jnp.float32),
    )
    key_piece = key_rows
    value_piece = values
    piece_rows = key_piece.shape[0]
    block_rows = math.gcd(piece_rows, 1024)

    def one_step(block_index, carry_state):
        run_max, run_sum, accumulated = carry_state
        key_block = lax.dynamic_slice_in_dim(
            key_piece, block_index * block_rows, block_rows, 0
        ).reshape(block_rows, head_count, head_width)
        value_block = lax.dynamic_slice_in_dim(
            value_piece, block_index * block_rows, block_rows, 0
        ).reshape(block_rows, head_count, head_width)
        scores = (
            jnp.einsum("qhd,khd->hqk", query_heads, key_block, preferred_element_type=jnp.float32)
            * scale
        )
        new_max = jnp.maximum(run_max, jnp.max(scores, axis=2))
        shrink = jnp.exp(run_max - new_max)
        raised = jnp.exp(scores - new_max[:, :, None])
        run_sum = run_sum * shrink + jnp.sum(raised, axis=2)
        accumulated = accumulated * shrink[:, :, None] + jnp.einsum(
            "hqk,khd->hqd",
            raised.astype(jnp.bfloat16),
            value_block,
            preferred_element_type=jnp.float32,
        )
        return (new_max, run_sum, accumulated)

    run_max, run_sum, accumulated = lax.fori_loop(0, piece_rows // block_rows, one_step, initial)
    attended = accumulated / run_sum[:, :, None]
    return (
        attended.transpose(1, 0, 2).reshape(row_count, head_count * head_width).astype(jnp.bfloat16)
    )


def slot_rank(owners_here, owner_count, group_rows):
    row_count = owners_here.shape[0]
    one_hot = (owners_here[:, None] == jnp.arange(owner_count, dtype=jnp.int32)[None, :]).astype(
        jnp.bfloat16
    )
    later_rows = lax.broadcasted_iota(jnp.int32, (row_count, row_count), 0)
    earlier_cols = lax.broadcasted_iota(jnp.int32, (row_count, row_count), 1)
    before = (
        (earlier_cols < later_rows) & (later_rows // group_rows == earlier_cols // group_rows)
    ).astype(jnp.bfloat16)
    counted = jnp.dot(before, one_hot, preferred_element_type=jnp.float32)
    return jnp.sum(counted * one_hot.astype(jnp.float32), axis=1)


def per_device(
    tokens,
    queries,
    key_rows,
    values,
    ssm_input,
    write_proj,
    read_proj,
    log_decay,
    attn_project,
    ssm_project,
    gauss_project,
    tile_owner,
):
    row_count = queries.shape[0]
    head_count = queries.shape[1] // HDIM

    def spread(part):
        split = part.reshape(row_count, head_count, HDIM)
        return lax.all_to_all(split, "sb", split_axis=1, concat_axis=0, tiled=True)

    query_heads = spread(queries)
    pair = jnp.stack([spread(key_rows), spread(values)]).reshape(2, -1, HDIM)
    gathered = lax.all_gather(pair, "sa", axis=1, tiled=True)
    group_keys = gathered[0]
    group_values = gathered[1]
    attended_one = fold_keys(query_heads, group_keys, group_values)
    attended = lax.all_to_all(
        attended_one.reshape(-1, 1, HDIM), "sb", split_axis=0, concat_axis=1, tiled=True
    ).reshape(row_count, head_count * HDIM)
    cumulative, inner_part, local_state, total_decay = chain_pieces(
        ssm_input, write_proj, read_proj, log_decay
    )
    entering = pass_states(local_state, total_decay)
    ssm_mix = chain_output(cumulative, inner_part, entering, read_proj)
    owner_count = lax.axis_size("head")
    own_index = lax.axis_index("head")
    sub_rows = row_count // owner_count
    capacity = sub_rows // 2
    width_out = gauss_project.shape[1]
    slot_count = owner_count * capacity
    slot_ids = jnp.arange(slot_count, dtype=jnp.float32)
    update = lax.psum_scatter(
        (
            jnp.dot(attended, attn_project, preferred_element_type=jnp.float32)
            + jnp.dot(ssm_mix, ssm_project, preferred_element_type=jnp.float32)
        ).astype(jnp.bfloat16),
        "head",
        scatter_dimension=0,
        tiled=True,
    ).astype(jnp.float32)
    own_tokens = lax.dynamic_slice_in_dim(tokens, own_index * sub_rows, sub_rows, 0)
    block_out = (own_tokens.astype(jnp.float32) + update).astype(jnp.bfloat16)
    gaussians = jnp.dot(block_out, gauss_project, preferred_element_type=jnp.float32).astype(
        jnp.bfloat16
    )
    owners_here = lax.dynamic_slice_in_dim(tile_owner, own_index * sub_rows, sub_rows, 0)
    slot_value = owners_here.astype(jnp.float32) * capacity + slot_rank(
        owners_here, owner_count, sub_rows
    )
    selector = (slot_ids[:, None] == slot_value[None, :]).astype(jnp.bfloat16)
    packed = jnp.dot(selector, gaussians, preferred_element_type=jnp.float32).astype(jnp.bfloat16)
    packed = packed.reshape(owner_count, capacity, width_out)
    received = lax.all_to_all(packed, "head", split_axis=0, concat_axis=0, tiled=True)
    tile_rows = received.reshape(1, 1, owner_count, capacity, width_out)
    return (block_out, tile_rows)


def solution(mesh):
    seq_count = mesh.shape["seq"]
    outer = math.gcd(seq_count, mesh.shape["head"])
    split_mesh = Mesh(
        mesh.devices.reshape(outer, seq_count // outer, mesh.shape["head"]), ("sb", "sa", "head")
    )
    seq = ("sb", "sa")
    in_specs = (
        P(seq, None),
        P(seq, "head"),
        P(seq, "head"),
        P(seq, "head"),
        P(seq, "head"),
        P(seq, None),
        P(seq, None),
        P("head", seq),
        P("head", None),
        P("head", None),
        P(),
        P(seq),
    )
    out_specs = (P(("sb", "sa", "head"), None), P(seq, "head", None, None, None))
    return jax.shard_map(
        per_device, mesh=split_mesh, in_specs=in_specs, out_specs=out_specs, check_vma=False
    )
```

```python
import math

import jax
import jax.numpy as jnp
from jax import lax
from jax.experimental import pallas as pl
from jax.experimental.pallas import tpu as pltpu
from jax.sharding import Mesh, PartitionSpec as P

HDIM = 64


def chain_pieces(ssm_input, write_proj, read_proj, log_decay):
    row_count = write_proj.shape[0]
    head_count = log_decay.shape[0]
    head_width = ssm_input.shape[1] // head_count
    cumulative = jnp.cumsum(log_decay, axis=1)
    inputs_heads = ssm_input.reshape(row_count, head_count, head_width)
    later_rows = lax.broadcasted_iota(jnp.int32, (row_count, row_count), 0)
    earlier_cols = lax.broadcasted_iota(jnp.int32, (row_count, row_count), 1)
    log_gaps = cumulative[:, :, None] - cumulative[:, None, :]
    decays = jnp.exp(jnp.where((later_rows >= earlier_cols)[None], log_gaps, -jnp.inf))
    cross_terms = jnp.dot(read_proj, write_proj.T, preferred_element_type=jnp.float32)
    mixing = (decays * cross_terms[None]).astype(jnp.bfloat16)
    inner_part = jnp.einsum(
        "hts,shp->thp", mixing, inputs_heads, preferred_element_type=jnp.float32
    )
    tail_decay = jnp.exp(cumulative[:, -1:] - cumulative)
    tail_inputs = (inputs_heads.astype(jnp.float32) * tail_decay.T[:, :, None]).astype(jnp.bfloat16)
    local_state = jnp.einsum(
        "sn,shp->hnp", write_proj, tail_inputs, preferred_element_type=jnp.float32
    )
    total_decay = jnp.exp(cumulative[:, -1])
    return (cumulative, inner_part, local_state, total_decay)


def chain_output(cumulative, inner_part, entering, read_proj):
    entering_low = entering.astype(jnp.bfloat16)
    outer_part = jnp.einsum(
        "tn,hnp->thp", read_proj, entering_low, preferred_element_type=jnp.float32
    )
    mixture = inner_part + outer_part * jnp.exp(cumulative).T[:, :, None]
    scaled = mixture * lax.rsqrt(jnp.mean(mixture * mixture, axis=2, keepdims=True) + 1e-05)
    return scaled.reshape(scaled.shape[0], -1).astype(jnp.bfloat16)


def pass_states(local_state, total_decay):
    axis = ("sb", "sa")
    devices = lax.axis_size(axis)
    mine = lax.axis_index(axis)

    def shifted(tree, distance):
        pairs = [(j, j + distance) for j in range(devices - distance)]
        return jax.tree.map(lambda part: lax.ppermute(part, axis, pairs), tree)

    decay, state = shifted((total_decay, local_state), 1)
    first = mine >= 1
    decay = jnp.where(first, decay, jnp.ones_like(decay))
    state = jnp.where(first, state, jnp.zeros_like(state))
    distance = 1
    while distance < devices:
        earlier_decay, earlier_state = shifted((decay, state), distance)
        reached = mine >= distance
        new_decay = earlier_decay * decay
        new_state = decay[:, None, None] * earlier_state + state
        decay = jnp.where(reached, new_decay, decay)
        state = jnp.where(reached, new_state, state)
        distance *= 2
    return state


def flash_one_head(query_rows, pair, key_block=1024):
    row_count, width = query_rows.shape
    key_count = pair.shape[1]
    steps = key_count // key_block
    scale = 1.0 / math.sqrt(width)

    def kernel(q_ref, k_ref, v_ref, o_ref, top_ref, sum_ref, acc_ref):
        step = pl.program_id(0)

        @pl.when(step == 0)
        def _():
            top_ref[...] = jnp.full(top_ref.shape, -jnp.inf, jnp.float32)
            sum_ref[...] = jnp.zeros(sum_ref.shape, jnp.float32)
            acc_ref[...] = jnp.zeros(acc_ref.shape, jnp.float32)

        scores = lax.dot_general(
            q_ref[...], k_ref[...], (((1,), (1,)), ((), ())), preferred_element_type=jnp.float32
        ) * scale
        old_top = top_ref[...]
        new_top = jnp.maximum(old_top, jnp.max(scores, axis=1, keepdims=True))
        shrink = jnp.exp(old_top - new_top)
        raised = jnp.exp(scores - new_top)
        sum_ref[...] = sum_ref[...] * shrink + jnp.sum(raised, axis=1, keepdims=True)
        acc_ref[...] = acc_ref[...] * shrink + jnp.dot(
            raised.astype(jnp.bfloat16), v_ref[...], preferred_element_type=jnp.float32
        )
        top_ref[...] = new_top

        @pl.when(step == steps - 1)
        def _():
            o_ref[...] = (acc_ref[...] / sum_ref[...]).astype(o_ref.dtype)

    return pl.pallas_call(
        kernel,
        out_shape=jax.ShapeDtypeStruct((row_count, width), jnp.bfloat16),
        grid=(steps,),
        in_specs=[
            pl.BlockSpec((row_count, width), lambda j: (0, 0)),
            pl.BlockSpec((None, key_block, width), lambda j: (0, j, 0)),
            pl.BlockSpec((None, key_block, width), lambda j: (1, j, 0)),
        ],
        out_specs=pl.BlockSpec((row_count, width), lambda j: (0, 0)),
        scratch_shapes=[
            pltpu.VMEM((row_count, 1), jnp.float32),
            pltpu.VMEM((row_count, 1), jnp.float32),
            pltpu.VMEM((row_count, width), jnp.float32),
        ],
        compiler_params=pltpu.CompilerParams(dimension_semantics=("arbitrary",)),
    )(query_rows, pair, pair)


def slot_rank(owners_here, owner_count, group_rows):
    row_count = owners_here.shape[0]
    one_hot = (owners_here[:, None] == jnp.arange(owner_count, dtype=jnp.int32)[None, :]).astype(
        jnp.bfloat16
    )
    later_rows = lax.broadcasted_iota(jnp.int32, (row_count, row_count), 0)
    earlier_cols = lax.broadcasted_iota(jnp.int32, (row_count, row_count), 1)
    before = (
        (earlier_cols < later_rows) & (later_rows // group_rows == earlier_cols // group_rows)
    ).astype(jnp.bfloat16)
    counted = jnp.dot(before, one_hot, preferred_element_type=jnp.float32)
    return jnp.sum(counted * one_hot.astype(jnp.float32), axis=1)


def per_device(
    tokens,
    queries,
    key_rows,
    values,
    ssm_input,
    write_proj,
    read_proj,
    log_decay,
    attn_project,
    ssm_project,
    gauss_project,
    tile_owner,
):
    row_count = queries.shape[0]
    head_count = queries.shape[1] // HDIM

    def spread(part):
        split = part.reshape(row_count, head_count, HDIM)
        return lax.all_to_all(split, "sb", split_axis=1, concat_axis=0, tiled=True)

    query_heads = spread(queries)
    pair = jnp.stack([spread(key_rows), spread(values)]).reshape(2, -1, HDIM)
    gathered = lax.all_gather(pair, "sa", axis=1, tiled=True)
    attended_one = flash_one_head(query_heads.reshape(-1, HDIM), gathered)
    attended = lax.all_to_all(
        attended_one.reshape(-1, 1, HDIM), "sb", split_axis=0, concat_axis=1, tiled=True
    ).reshape(row_count, head_count * HDIM)
    cumulative, inner_part, local_state, total_decay = chain_pieces(
        ssm_input, write_proj, read_proj, log_decay
    )
    entering = pass_states(local_state, total_decay)
    ssm_mix = chain_output(cumulative, inner_part, entering, read_proj)
    owner_count = lax.axis_size("head")
    own_index = lax.axis_index("head")
    sub_rows = row_count // owner_count
    capacity = sub_rows // 2
    width_out = gauss_project.shape[1]
    slot_count = owner_count * capacity
    slot_ids = jnp.arange(slot_count, dtype=jnp.float32)
    update = lax.psum_scatter(
        (
            jnp.dot(attended, attn_project, preferred_element_type=jnp.float32)
            + jnp.dot(ssm_mix, ssm_project, preferred_element_type=jnp.float32)
        ).astype(jnp.bfloat16),
        "head",
        scatter_dimension=0,
        tiled=True,
    ).astype(jnp.float32)
    own_tokens = lax.dynamic_slice_in_dim(tokens, own_index * sub_rows, sub_rows, 0)
    block_out = (own_tokens.astype(jnp.float32) + update).astype(jnp.bfloat16)
    gaussians = jnp.dot(block_out, gauss_project, preferred_element_type=jnp.float32).astype(
        jnp.bfloat16
    )
    owners_here = lax.dynamic_slice_in_dim(tile_owner, own_index * sub_rows, sub_rows, 0)
    slot_value = owners_here.astype(jnp.float32) * capacity + slot_rank(
        owners_here, owner_count, sub_rows
    )
    selector = (slot_ids[:, None] == slot_value[None, :]).astype(jnp.bfloat16)
    packed = jnp.dot(selector, gaussians, preferred_element_type=jnp.float32).astype(jnp.bfloat16)
    packed = packed.reshape(owner_count, capacity, width_out)
    received = lax.all_to_all(packed, "head", split_axis=0, concat_axis=0, tiled=True)
    tile_rows = received.reshape(1, 1, owner_count, capacity, width_out)
    return (block_out, tile_rows)


def solution(mesh):
    seq_count = mesh.shape["seq"]
    outer = math.gcd(seq_count, mesh.shape["head"])
    split_mesh = Mesh(
        mesh.devices.reshape(outer, seq_count // outer, mesh.shape["head"]), ("sb", "sa", "head")
    )
    seq = ("sb", "sa")
    in_specs = (
        P(seq, None),
        P(seq, "head"),
        P(seq, "head"),
        P(seq, "head"),
        P(seq, "head"),
        P(seq, None),
        P(seq, None),
        P("head", seq),
        P("head", None),
        P("head", None),
        P(),
        P(seq),
    )
    out_specs = (P(("sb", "sa", "head"), None), P(seq, "head", None, None, None))
    return jax.shard_map(
        per_device, mesh=split_mesh, in_specs=in_specs, out_specs=out_specs, check_vma=False
    )
```

```python
import math

import jax
import jax.numpy as jnp
from jax import lax
from jax.experimental import pallas as pl
from jax.experimental.pallas import tpu as pltpu
from jax.sharding import Mesh, PartitionSpec as P

HDIM = 64


def chain_pieces(ssm_input, write_proj, read_proj, log_decay):
    row_count = write_proj.shape[0]
    head_count = log_decay.shape[0]
    head_width = ssm_input.shape[1] // head_count
    cumulative = jnp.cumsum(log_decay, axis=1)
    inputs_heads = ssm_input.reshape(row_count, head_count, head_width)
    later_rows = lax.broadcasted_iota(jnp.int32, (row_count, row_count), 0)
    earlier_cols = lax.broadcasted_iota(jnp.int32, (row_count, row_count), 1)
    log_gaps = cumulative[:, :, None] - cumulative[:, None, :]
    decays = jnp.exp(jnp.where((later_rows >= earlier_cols)[None], log_gaps, -jnp.inf))
    cross_terms = jnp.dot(read_proj, write_proj.T, preferred_element_type=jnp.float32)
    mixing = (decays * cross_terms[None]).astype(jnp.bfloat16)
    inner_part = jnp.einsum(
        "hts,shp->thp", mixing, inputs_heads, preferred_element_type=jnp.float32
    )
    tail_decay = jnp.exp(cumulative[:, -1:] - cumulative)
    tail_inputs = (inputs_heads.astype(jnp.float32) * tail_decay.T[:, :, None]).astype(jnp.bfloat16)
    local_state = jnp.einsum(
        "sn,shp->hnp", write_proj, tail_inputs, preferred_element_type=jnp.float32
    )
    total_decay = jnp.exp(cumulative[:, -1])
    return (cumulative, inner_part, local_state, total_decay)


def chain_output(cumulative, inner_part, entering, read_proj):
    entering_low = entering.astype(jnp.bfloat16)
    outer_part = jnp.einsum(
        "tn,hnp->thp", read_proj, entering_low, preferred_element_type=jnp.float32
    )
    mixture = inner_part + outer_part * jnp.exp(cumulative).T[:, :, None]
    scaled = mixture * lax.rsqrt(jnp.mean(mixture * mixture, axis=2, keepdims=True) + 1e-05)
    return scaled.reshape(scaled.shape[0], -1).astype(jnp.bfloat16)


def pass_states(local_state, total_decay):
    axis = ("sb", "sa")
    devices = lax.axis_size(axis)
    mine = lax.axis_index(axis)

    def shifted(tree, distance):
        pairs = [(j, j + distance) for j in range(devices - distance)]
        return jax.tree.map(lambda part: lax.ppermute(part, axis, pairs), tree)

    decay, state = shifted((total_decay, local_state), 1)
    first = mine >= 1
    decay = jnp.where(first, decay, jnp.ones_like(decay))
    state = jnp.where(first, state, jnp.zeros_like(state))
    distance = 1
    while distance < devices:
        earlier_decay, earlier_state = shifted((decay, state), distance)
        reached = mine >= distance
        new_decay = earlier_decay * decay
        new_state = decay[:, None, None] * earlier_state + state
        decay = jnp.where(reached, new_decay, decay)
        state = jnp.where(reached, new_state, state)
        distance *= 2
    return state


def flash_one_head(query_rows, pair_t, key_block=4096):
    row_count, width = query_rows.shape
    key_count = pair_t.shape[2]
    steps = key_count // key_block
    scale = 1.0 / math.sqrt(width)

    def kernel(q_ref, k_ref, v_ref, o_ref, top_ref, sum_ref, acc_ref):
        step = pl.program_id(0)

        @pl.when(step == 0)
        def _():
            top_ref[...] = jnp.full(top_ref.shape, -jnp.inf, jnp.float32)
            sum_ref[...] = jnp.zeros(sum_ref.shape, jnp.float32)
            acc_ref[...] = jnp.zeros(acc_ref.shape, jnp.float32)

        scores = jnp.dot(q_ref[...], k_ref[...], preferred_element_type=jnp.float32) * scale
        old_top = top_ref[...]
        new_top = jnp.maximum(old_top, jnp.max(scores, axis=1, keepdims=True))
        shrink = jnp.exp(old_top - new_top)
        raised = jnp.exp(scores - new_top)
        sum_ref[...] = sum_ref[...] * shrink + jnp.sum(raised, axis=1, keepdims=True)
        acc_ref[...] = acc_ref[...] * shrink + lax.dot_general(
            raised.astype(jnp.bfloat16),
            v_ref[...],
            (((1,), (1,)), ((), ())),
            preferred_element_type=jnp.float32,
        )
        top_ref[...] = new_top

        @pl.when(step == steps - 1)
        def _():
            o_ref[...] = (acc_ref[...] / sum_ref[...]).astype(o_ref.dtype)

    return pl.pallas_call(
        kernel,
        out_shape=jax.ShapeDtypeStruct((row_count, width), jnp.bfloat16),
        grid=(steps,),
        in_specs=[
            pl.BlockSpec((row_count, width), lambda j: (0, 0)),
            pl.BlockSpec((None, width, key_block), lambda j: (0, 0, j)),
            pl.BlockSpec((None, width, key_block), lambda j: (1, 0, j)),
        ],
        out_specs=pl.BlockSpec((row_count, width), lambda j: (0, 0)),
        scratch_shapes=[
            pltpu.VMEM((row_count, 1), jnp.float32),
            pltpu.VMEM((row_count, 1), jnp.float32),
            pltpu.VMEM((row_count, width), jnp.float32),
        ],
        compiler_params=pltpu.CompilerParams(dimension_semantics=("arbitrary",)),
    )(query_rows, pair_t, pair_t)


def slot_rank(owners_here, owner_count, group_rows):
    row_count = owners_here.shape[0]
    one_hot = (owners_here[:, None] == jnp.arange(owner_count, dtype=jnp.int32)[None, :]).astype(
        jnp.bfloat16
    )
    later_rows = lax.broadcasted_iota(jnp.int32, (row_count, row_count), 0)
    earlier_cols = lax.broadcasted_iota(jnp.int32, (row_count, row_count), 1)
    before = (
        (earlier_cols < later_rows) & (later_rows // group_rows == earlier_cols // group_rows)
    ).astype(jnp.bfloat16)
    counted = jnp.dot(before, one_hot, preferred_element_type=jnp.float32)
    return jnp.sum(counted * one_hot.astype(jnp.float32), axis=1)


def per_device(
    tokens,
    queries,
    key_rows,
    values,
    ssm_input,
    write_proj,
    read_proj,
    log_decay,
    attn_project,
    ssm_project,
    gauss_project,
    tile_owner,
):
    row_count = queries.shape[0]
    head_count = queries.shape[1] // HDIM

    def spread(part):
        split = part.reshape(row_count, head_count, HDIM)
        return lax.all_to_all(split, "sb", split_axis=1, concat_axis=0, tiled=True)

    query_heads = spread(queries)
    pair_t = jnp.stack(
        [spread(key_rows).reshape(-1, HDIM).T, spread(values).reshape(-1, HDIM).T]
    )
    gathered = lax.all_gather(pair_t, "sa", axis=2, tiled=True)
    attended_one = flash_one_head(query_heads.reshape(-1, HDIM), gathered)
    attended = lax.all_to_all(
        attended_one.reshape(-1, 1, HDIM), "sb", split_axis=0, concat_axis=1, tiled=True
    ).reshape(row_count, head_count * HDIM)
    cumulative, inner_part, local_state, total_decay = chain_pieces(
        ssm_input, write_proj, read_proj, log_decay
    )
    entering = pass_states(local_state, total_decay)
    ssm_mix = chain_output(cumulative, inner_part, entering, read_proj)
    owner_count = lax.axis_size("head")
    own_index = lax.axis_index("head")
    sub_rows = row_count // owner_count
    capacity = sub_rows // 2
    width_out = gauss_project.shape[1]
    slot_count = owner_count * capacity
    slot_ids = jnp.arange(slot_count, dtype=jnp.float32)
    update = lax.psum_scatter(
        (
            jnp.dot(attended, attn_project, preferred_element_type=jnp.float32)
            + jnp.dot(ssm_mix, ssm_project, preferred_element_type=jnp.float32)
        ).astype(jnp.bfloat16),
        "head",
        scatter_dimension=0,
        tiled=True,
    ).astype(jnp.float32)
    own_tokens = lax.dynamic_slice_in_dim(tokens, own_index * sub_rows, sub_rows, 0)
    block_out = (own_tokens.astype(jnp.float32) + update).astype(jnp.bfloat16)
    gaussians = jnp.dot(block_out, gauss_project, preferred_element_type=jnp.float32).astype(
        jnp.bfloat16
    )
    owners_here = lax.dynamic_slice_in_dim(tile_owner, own_index * sub_rows, sub_rows, 0)
    slot_value = owners_here.astype(jnp.float32) * capacity + slot_rank(
        owners_here, owner_count, sub_rows
    )
    selector = (slot_ids[:, None] == slot_value[None, :]).astype(jnp.bfloat16)
    packed = jnp.dot(selector, gaussians, preferred_element_type=jnp.float32).astype(jnp.bfloat16)
    packed = packed.reshape(owner_count, capacity, width_out)
    received = lax.all_to_all(packed, "head", split_axis=0, concat_axis=0, tiled=True)
    tile_rows = received.reshape(1, 1, owner_count, capacity, width_out)
    return (block_out, tile_rows)


def solution(mesh):
    seq_count = mesh.shape["seq"]
    outer = math.gcd(seq_count, mesh.shape["head"])
    split_mesh = Mesh(
        mesh.devices.reshape(outer, seq_count // outer, mesh.shape["head"]), ("sb", "sa", "head")
    )
    seq = ("sb", "sa")
    in_specs = (
        P(seq, None),
        P(seq, "head"),
        P(seq, "head"),
        P(seq, "head"),
        P(seq, "head"),
        P(seq, None),
        P(seq, None),
        P("head", seq),
        P("head", None),
        P("head", None),
        P(),
        P(seq),
    )
    out_specs = (P(("sb", "sa", "head"), None), P(seq, "head", None, None, None))
    return jax.shard_map(
        per_device, mesh=split_mesh, in_specs=in_specs, out_specs=out_specs, check_vma=False
    )
```

```python
import math

import jax
import jax.numpy as jnp
from jax import lax
from jax.experimental import pallas as pl
from jax.experimental.pallas import tpu as pltpu
from jax.sharding import Mesh, PartitionSpec as P

HDIM = 64


def chain_pieces(ssm_input, write_proj, read_proj, log_decay):
    row_count = write_proj.shape[0]
    head_count = log_decay.shape[0]
    head_width = ssm_input.shape[1] // head_count
    cumulative = jnp.cumsum(log_decay, axis=1)
    inputs_heads = ssm_input.reshape(row_count, head_count, head_width)
    later_rows = lax.broadcasted_iota(jnp.int32, (row_count, row_count), 0)
    earlier_cols = lax.broadcasted_iota(jnp.int32, (row_count, row_count), 1)
    log_gaps = cumulative[:, :, None] - cumulative[:, None, :]
    decays = jnp.exp(jnp.where((later_rows >= earlier_cols)[None], log_gaps, -jnp.inf))
    cross_terms = jnp.dot(read_proj, write_proj.T, preferred_element_type=jnp.float32)
    mixing = (decays * cross_terms[None]).astype(jnp.bfloat16)
    inner_part = jnp.einsum(
        "hts,shp->thp", mixing, inputs_heads, preferred_element_type=jnp.float32
    )
    tail_decay = jnp.exp(cumulative[:, -1:] - cumulative)
    tail_inputs = (inputs_heads.astype(jnp.float32) * tail_decay.T[:, :, None]).astype(jnp.bfloat16)
    local_state = jnp.einsum(
        "sn,shp->hnp", write_proj, tail_inputs, preferred_element_type=jnp.float32
    )
    total_decay = jnp.exp(cumulative[:, -1])
    return (cumulative, inner_part, local_state, total_decay)


def chain_output(cumulative, inner_part, entering, read_proj):
    entering_low = entering.astype(jnp.bfloat16)
    outer_part = jnp.einsum(
        "tn,hnp->thp", read_proj, entering_low, preferred_element_type=jnp.float32
    )
    mixture = inner_part + outer_part * jnp.exp(cumulative).T[:, :, None]
    scaled = mixture * lax.rsqrt(jnp.mean(mixture * mixture, axis=2, keepdims=True) + 1e-05)
    return scaled.reshape(scaled.shape[0], -1).astype(jnp.bfloat16)


def pass_states(local_state, total_decay):
    axis = ("sb", "sa")
    devices = lax.axis_size(axis)
    mine = lax.axis_index(axis)
    head_count, state_rows, width = local_state.shape
    decay_rows = jnp.broadcast_to(total_decay[:, None, None], (head_count, 8, width))
    packed = jnp.concatenate([local_state, decay_rows], axis=1)

    def shifted(part, distance):
        pairs = [(j, j + distance) for j in range(devices - distance)]
        return lax.ppermute(part, axis, pairs)

    identity = jnp.concatenate(
        [jnp.zeros_like(local_state), jnp.ones_like(decay_rows)], axis=1
    )
    packed = jnp.where(mine >= 1, shifted(packed, 1), identity)
    distance = 1
    while distance < devices:
        earlier = shifted(packed, distance)
        decay = packed[:, state_rows:state_rows + 1, :1]
        combined = jnp.concatenate(
            [
                decay * earlier[:, :state_rows] + packed[:, :state_rows],
                earlier[:, state_rows:] * packed[:, state_rows:],
            ],
            axis=1,
        )
        packed = jnp.where(mine >= distance, combined, packed)
        distance *= 2
    return packed[:, :state_rows]


def flash_one_head(query_rows, pair_t, key_block=4096):
    row_count, width = query_rows.shape
    key_count = pair_t.shape[2]
    steps = key_count // key_block
    scale = 1.0 / math.sqrt(width)

    def kernel(q_ref, k_ref, v_ref, o_ref, top_ref, sum_ref, acc_ref):
        step = pl.program_id(0)

        @pl.when(step == 0)
        def _():
            top_ref[...] = jnp.full(top_ref.shape, -jnp.inf, jnp.float32)
            sum_ref[...] = jnp.zeros(sum_ref.shape, jnp.float32)
            acc_ref[...] = jnp.zeros(acc_ref.shape, jnp.float32)

        scores = jnp.dot(q_ref[...], k_ref[...], preferred_element_type=jnp.float32) * scale
        old_top = top_ref[...]
        new_top = jnp.maximum(old_top, jnp.max(scores, axis=1, keepdims=True))
        shrink = jnp.exp(old_top - new_top)
        raised = jnp.exp(scores - new_top)
        sum_ref[...] = sum_ref[...] * shrink + jnp.sum(raised, axis=1, keepdims=True)
        acc_ref[...] = acc_ref[...] * shrink + lax.dot_general(
            raised.astype(jnp.bfloat16),
            v_ref[...],
            (((1,), (1,)), ((), ())),
            preferred_element_type=jnp.float32,
        )
        top_ref[...] = new_top

        @pl.when(step == steps - 1)
        def _():
            o_ref[...] = (acc_ref[...] / sum_ref[...]).astype(o_ref.dtype)

    return pl.pallas_call(
        kernel,
        out_shape=jax.ShapeDtypeStruct((row_count, width), jnp.bfloat16),
        grid=(steps,),
        in_specs=[
            pl.BlockSpec((row_count, width), lambda j: (0, 0)),
            pl.BlockSpec((None, width, key_block), lambda j: (0, 0, j)),
            pl.BlockSpec((None, width, key_block), lambda j: (1, 0, j)),
        ],
        out_specs=pl.BlockSpec((row_count, width), lambda j: (0, 0)),
        scratch_shapes=[
            pltpu.VMEM((row_count, 1), jnp.float32),
            pltpu.VMEM((row_count, 1), jnp.float32),
            pltpu.VMEM((row_count, width), jnp.float32),
        ],
        compiler_params=pltpu.CompilerParams(dimension_semantics=("arbitrary",)),
    )(query_rows, pair_t, pair_t)


def slot_rank(owners_here, owner_count, group_rows):
    row_count = owners_here.shape[0]
    one_hot = (owners_here[:, None] == jnp.arange(owner_count, dtype=jnp.int32)[None, :]).astype(
        jnp.bfloat16
    )
    later_rows = lax.broadcasted_iota(jnp.int32, (row_count, row_count), 0)
    earlier_cols = lax.broadcasted_iota(jnp.int32, (row_count, row_count), 1)
    before = (
        (earlier_cols < later_rows) & (later_rows // group_rows == earlier_cols // group_rows)
    ).astype(jnp.bfloat16)
    counted = jnp.dot(before, one_hot, preferred_element_type=jnp.float32)
    return jnp.sum(counted * one_hot.astype(jnp.float32), axis=1)


def per_device(
    tokens,
    queries,
    key_rows,
    values,
    ssm_input,
    write_proj,
    read_proj,
    log_decay,
    attn_project,
    ssm_project,
    gauss_project,
    tile_owner,
):
    row_count = queries.shape[0]
    head_count = queries.shape[1] // HDIM

    def spread(part):
        split = part.reshape(row_count, head_count, HDIM)
        return lax.all_to_all(split, "sb", split_axis=1, concat_axis=0, tiled=True)

    query_heads = spread(queries)
    pair_t = jnp.stack(
        [spread(key_rows).reshape(-1, HDIM).T, spread(values).reshape(-1, HDIM).T]
    )
    gathered = lax.all_gather(pair_t, "sa", axis=2, tiled=True)
    attended_one = flash_one_head(query_heads.reshape(-1, HDIM), gathered)
    attended = lax.all_to_all(
        attended_one.reshape(-1, 1, HDIM), "sb", split_axis=0, concat_axis=1, tiled=True
    ).reshape(row_count, head_count * HDIM)
    cumulative, inner_part, local_state, total_decay = chain_pieces(
        ssm_input, write_proj, read_proj, log_decay
    )
    entering = pass_states(local_state, total_decay)
    ssm_mix = chain_output(cumulative, inner_part, entering, read_proj)
    owner_count = lax.axis_size("head")
    own_index = lax.axis_index("head")
    sub_rows = row_count // owner_count
    capacity = sub_rows // 2
    width_out = gauss_project.shape[1]
    slot_count = owner_count * capacity
    slot_ids = jnp.arange(slot_count, dtype=jnp.float32)
    update = lax.psum_scatter(
        (
            jnp.dot(attended, attn_project, preferred_element_type=jnp.float32)
            + jnp.dot(ssm_mix, ssm_project, preferred_element_type=jnp.float32)
        ).astype(jnp.bfloat16),
        "head",
        scatter_dimension=0,
        tiled=True,
    ).astype(jnp.float32)
    own_tokens = lax.dynamic_slice_in_dim(tokens, own_index * sub_rows, sub_rows, 0)
    block_out = (own_tokens.astype(jnp.float32) + update).astype(jnp.bfloat16)
    gaussians = jnp.dot(block_out, gauss_project, preferred_element_type=jnp.float32).astype(
        jnp.bfloat16
    )
    owners_here = lax.dynamic_slice_in_dim(tile_owner, own_index * sub_rows, sub_rows, 0)
    slot_value = owners_here.astype(jnp.float32) * capacity + slot_rank(
        owners_here, owner_count, sub_rows
    )
    selector = (slot_ids[:, None] == slot_value[None, :]).astype(jnp.bfloat16)
    packed = jnp.dot(selector, gaussians, preferred_element_type=jnp.float32).astype(jnp.bfloat16)
    packed = packed.reshape(owner_count, capacity, width_out)
    received = lax.all_to_all(packed, "head", split_axis=0, concat_axis=0, tiled=True)
    tile_rows = received.reshape(1, 1, owner_count, capacity, width_out)
    return (block_out, tile_rows)


def solution(mesh):
    seq_count = mesh.shape["seq"]
    outer = math.gcd(seq_count, mesh.shape["head"])
    split_mesh = Mesh(
        mesh.devices.reshape(outer, seq_count // outer, mesh.shape["head"]), ("sb", "sa", "head")
    )
    seq = ("sb", "sa")
    in_specs = (
        P(seq, None),
        P(seq, "head"),
        P(seq, "head"),
        P(seq, "head"),
        P(seq, "head"),
        P(seq, None),
        P(seq, None),
        P("head", seq),
        P("head", None),
        P("head", None),
        P(),
        P(seq),
    )
    out_specs = (P(("sb", "sa", "head"), None), P(seq, "head", None, None, None))
    return jax.shard_map(
        per_device, mesh=split_mesh, in_specs=in_specs, out_specs=out_specs, check_vma=False
    )
```

```python
import math

import jax
import jax.numpy as jnp
from jax import lax
from jax.experimental import pallas as pl
from jax.experimental.pallas import tpu as pltpu
from jax.sharding import Mesh, PartitionSpec as P

HDIM = 64


def chain_pieces(ssm_input, write_proj, read_proj, log_decay):
    row_count = write_proj.shape[0]
    head_count = log_decay.shape[0]
    head_width = ssm_input.shape[1] // head_count
    cumulative = jnp.cumsum(log_decay, axis=1)
    inputs_heads = ssm_input.reshape(row_count, head_count, head_width)
    later_rows = lax.broadcasted_iota(jnp.int32, (row_count, row_count), 0)
    earlier_cols = lax.broadcasted_iota(jnp.int32, (row_count, row_count), 1)
    log_gaps = cumulative[:, :, None] - cumulative[:, None, :]
    decays = jnp.exp(jnp.where((later_rows >= earlier_cols)[None], log_gaps, -jnp.inf))
    cross_terms = jnp.dot(read_proj, write_proj.T, preferred_element_type=jnp.float32)
    mixing = (decays * cross_terms[None]).astype(jnp.bfloat16)
    inner_part = jnp.einsum(
        "hts,shp->thp", mixing, inputs_heads, preferred_element_type=jnp.float32
    )
    tail_decay = jnp.exp(cumulative[:, -1:] - cumulative)
    tail_inputs = (inputs_heads.astype(jnp.float32) * tail_decay.T[:, :, None]).astype(jnp.bfloat16)
    local_state = jnp.einsum(
        "sn,shp->hnp", write_proj, tail_inputs, preferred_element_type=jnp.float32
    )
    total_decay = jnp.exp(cumulative[:, -1])
    return (cumulative, inner_part, local_state, total_decay)


def chain_output(cumulative, inner_part, entering, read_proj):
    entering_low = entering.astype(jnp.bfloat16)
    outer_part = jnp.einsum(
        "tn,hnp->thp", read_proj, entering_low, preferred_element_type=jnp.float32
    )
    mixture = inner_part + outer_part * jnp.exp(cumulative).T[:, :, None]
    scaled = mixture * lax.rsqrt(jnp.mean(mixture * mixture, axis=2, keepdims=True) + 1e-05)
    return scaled.reshape(scaled.shape[0], -1).astype(jnp.bfloat16)


def pass_states(local_state, total_decay):
    axis = ("sb", "sa")
    devices = lax.axis_size(axis)
    mine = lax.axis_index(axis)

    def shifted(tree, distance):
        pairs = [(j, j + distance) for j in range(devices - distance)]
        return jax.tree.map(lambda part: lax.ppermute(part, axis, pairs), tree)

    decay, state = shifted((total_decay, local_state), 1)
    first = mine >= 1
    decay = jnp.where(first, decay, jnp.ones_like(decay))
    state = jnp.where(first, state, jnp.zeros_like(state))
    distance = 1
    while distance < devices:
        earlier_decay, earlier_state = shifted((decay, state), distance)
        reached = mine >= distance
        new_decay = earlier_decay * decay
        new_state = decay[:, None, None] * earlier_state + state
        decay = jnp.where(reached, new_decay, decay)
        state = jnp.where(reached, new_state, state)
        distance *= 2
    return state


def flash_one_head_t(query_t, pair_t, key_block=4096):
    width, row_count = query_t.shape
    key_count = pair_t.shape[2]
    steps = key_count // key_block
    scale = 1.0 / math.sqrt(width)

    def kernel(q_ref, k_ref, v_ref, o_ref, top_ref, sum_ref, acc_ref):
        step = pl.program_id(0)

        @pl.when(step == 0)
        def _():
            top_ref[...] = jnp.full(top_ref.shape, -jnp.inf, jnp.float32)
            sum_ref[...] = jnp.zeros(sum_ref.shape, jnp.float32)
            acc_ref[...] = jnp.zeros(acc_ref.shape, jnp.float32)

        scores = lax.dot_general(
            k_ref[...], q_ref[...], (((0,), (0,)), ((), ())), preferred_element_type=jnp.float32
        ) * scale
        old_top = top_ref[...]
        new_top = jnp.maximum(old_top, jnp.max(scores, axis=0, keepdims=True))
        shrink = jnp.exp(old_top - new_top)
        raised = jnp.exp(scores - new_top)
        sum_ref[...] = sum_ref[...] * shrink + jnp.sum(raised, axis=0, keepdims=True)
        acc_ref[...] = acc_ref[...] * shrink + jnp.dot(
            v_ref[...], raised.astype(jnp.bfloat16), preferred_element_type=jnp.float32
        )
        top_ref[...] = new_top

        @pl.when(step == steps - 1)
        def _():
            o_ref[...] = (acc_ref[...] / sum_ref[...]).astype(o_ref.dtype)

    return pl.pallas_call(
        kernel,
        out_shape=jax.ShapeDtypeStruct((width, row_count), jnp.bfloat16),
        grid=(steps,),
        in_specs=[
            pl.BlockSpec((width, row_count), lambda j: (0, 0)),
            pl.BlockSpec((None, width, key_block), lambda j: (0, 0, j)),
            pl.BlockSpec((None, width, key_block), lambda j: (1, 0, j)),
        ],
        out_specs=pl.BlockSpec((width, row_count), lambda j: (0, 0)),
        scratch_shapes=[
            pltpu.VMEM((1, row_count), jnp.float32),
            pltpu.VMEM((1, row_count), jnp.float32),
            pltpu.VMEM((width, row_count), jnp.float32),
        ],
        compiler_params=pltpu.CompilerParams(dimension_semantics=("arbitrary",)),
    )(query_t, pair_t, pair_t)


def slot_rank(owners_here, owner_count, group_rows):
    row_count = owners_here.shape[0]
    one_hot = (owners_here[:, None] == jnp.arange(owner_count, dtype=jnp.int32)[None, :]).astype(
        jnp.bfloat16
    )
    later_rows = lax.broadcasted_iota(jnp.int32, (row_count, row_count), 0)
    earlier_cols = lax.broadcasted_iota(jnp.int32, (row_count, row_count), 1)
    before = (
        (earlier_cols < later_rows) & (later_rows // group_rows == earlier_cols // group_rows)
    ).astype(jnp.bfloat16)
    counted = jnp.dot(before, one_hot, preferred_element_type=jnp.float32)
    return jnp.sum(counted * one_hot.astype(jnp.float32), axis=1)


def per_device(
    tokens,
    queries,
    key_rows,
    values,
    ssm_input,
    write_proj,
    read_proj,
    log_decay,
    attn_project,
    ssm_project,
    gauss_project,
    tile_owner,
):
    row_count = queries.shape[0]
    head_count = queries.shape[1] // HDIM

    def spread(part):
        split = part.reshape(row_count, head_count, HDIM)
        return lax.all_to_all(split, "sb", split_axis=1, concat_axis=0, tiled=True)

    query_heads = spread(queries)
    pair_t = jnp.stack(
        [spread(key_rows).reshape(-1, HDIM).T, spread(values).reshape(-1, HDIM).T]
    )
    gathered = lax.all_gather(pair_t, "sa", axis=2, tiled=True)
    attended_one = flash_one_head_t(query_heads.reshape(-1, HDIM).T, gathered).T
    attended = lax.all_to_all(
        attended_one.reshape(-1, 1, HDIM), "sb", split_axis=0, concat_axis=1, tiled=True
    ).reshape(row_count, head_count * HDIM)
    cumulative, inner_part, local_state, total_decay = chain_pieces(
        ssm_input, write_proj, read_proj, log_decay
    )
    entering = pass_states(local_state, total_decay)
    ssm_mix = chain_output(cumulative, inner_part, entering, read_proj)
    owner_count = lax.axis_size("head")
    own_index = lax.axis_index("head")
    sub_rows = row_count // owner_count
    capacity = sub_rows // 2
    width_out = gauss_project.shape[1]
    slot_count = owner_count * capacity
    slot_ids = jnp.arange(slot_count, dtype=jnp.float32)
    partial = (
        jnp.dot(attended, attn_project, preferred_element_type=jnp.float32)
        + jnp.dot(ssm_mix, ssm_project, preferred_element_type=jnp.float32)
    ).astype(jnp.bfloat16)
    pieces = lax.all_to_all(
        partial.reshape(owner_count, sub_rows, partial.shape[1]),
        "head",
        split_axis=0,
        concat_axis=0,
        tiled=True,
    )
    update = jnp.sum(pieces.astype(jnp.float32), axis=0)
    own_tokens = lax.dynamic_slice_in_dim(tokens, own_index * sub_rows, sub_rows, 0)
    block_out = (own_tokens.astype(jnp.float32) + update).astype(jnp.bfloat16)
    gaussians = jnp.dot(block_out, gauss_project, preferred_element_type=jnp.float32).astype(
        jnp.bfloat16
    )
    owners_here = lax.dynamic_slice_in_dim(tile_owner, own_index * sub_rows, sub_rows, 0)
    slot_value = owners_here.astype(jnp.float32) * capacity + slot_rank(
        owners_here, owner_count, sub_rows
    )
    selector = (slot_ids[:, None] == slot_value[None, :]).astype(jnp.bfloat16)
    packed = jnp.dot(selector, gaussians, preferred_element_type=jnp.float32).astype(jnp.bfloat16)
    packed = packed.reshape(owner_count, capacity, width_out)
    received = lax.all_to_all(packed, "head", split_axis=0, concat_axis=0, tiled=True)
    tile_rows = received.reshape(1, 1, owner_count, capacity, width_out)
    return (block_out, tile_rows)


def solution(mesh):
    seq_count = mesh.shape["seq"]
    outer = math.gcd(seq_count, mesh.shape["head"])
    split_mesh = Mesh(
        mesh.devices.reshape(outer, seq_count // outer, mesh.shape["head"]), ("sb", "sa", "head")
    )
    seq = ("sb", "sa")
    in_specs = (
        P(seq, None),
        P(seq, "head"),
        P(seq, "head"),
        P(seq, "head"),
        P(seq, "head"),
        P(seq, None),
        P(seq, None),
        P("head", seq),
        P("head", None),
        P("head", None),
        P(),
        P(seq),
    )
    out_specs = (P(("sb", "sa", "head"), None), P(seq, "head", None, None, None))
    return jax.shard_map(
        per_device, mesh=split_mesh, in_specs=in_specs, out_specs=out_specs, check_vma=False
    )
```

```python
import math

import jax
import jax.numpy as jnp
from jax import lax
from jax.experimental import pallas as pl
from jax.experimental.pallas import tpu as pltpu
from jax.sharding import Mesh, PartitionSpec as P

HDIM = 64


def chain_pieces(ssm_input, write_proj, read_proj, log_decay):
    row_count = write_proj.shape[0]
    head_count = log_decay.shape[0]
    head_width = ssm_input.shape[1] // head_count
    cumulative = jnp.cumsum(log_decay, axis=1)
    inputs_heads = ssm_input.reshape(row_count, head_count, head_width)
    later_rows = lax.broadcasted_iota(jnp.int32, (row_count, row_count), 0)
    earlier_cols = lax.broadcasted_iota(jnp.int32, (row_count, row_count), 1)
    log_gaps = cumulative[:, :, None] - cumulative[:, None, :]
    decays = jnp.exp(jnp.where((later_rows >= earlier_cols)[None], log_gaps, -jnp.inf))
    cross_terms = jnp.dot(read_proj, write_proj.T, preferred_element_type=jnp.float32)
    mixing = (decays * cross_terms[None]).astype(jnp.bfloat16)
    inner_part = jnp.einsum(
        "hts,shp->thp", mixing, inputs_heads, preferred_element_type=jnp.float32
    )
    tail_decay = jnp.exp(cumulative[:, -1:] - cumulative)
    tail_inputs = (inputs_heads.astype(jnp.float32) * tail_decay.T[:, :, None]).astype(jnp.bfloat16)
    local_state = jnp.einsum(
        "sn,shp->hnp", write_proj, tail_inputs, preferred_element_type=jnp.float32
    )
    total_decay = jnp.exp(cumulative[:, -1])
    return (cumulative, inner_part, local_state, total_decay)


def chain_output(cumulative, inner_part, entering, read_proj):
    entering_low = entering.astype(jnp.bfloat16)
    outer_part = jnp.einsum(
        "tn,hnp->thp", read_proj, entering_low, preferred_element_type=jnp.float32
    )
    mixture = inner_part + outer_part * jnp.exp(cumulative).T[:, :, None]
    scaled = mixture * lax.rsqrt(jnp.mean(mixture * mixture, axis=2, keepdims=True) + 1e-05)
    return scaled.reshape(scaled.shape[0], -1).astype(jnp.bfloat16)


def pass_states(local_state, total_decay):
    axis = ("sb", "sy", "sz")
    devices = lax.axis_size(axis)
    mine = lax.axis_index(axis)

    def shifted(tree, distance):
        pairs = [(j, j + distance) for j in range(devices - distance)]
        return jax.tree.map(lambda part: lax.ppermute(part, axis, pairs), tree)

    decay, state = shifted((total_decay, local_state), 1)
    first = mine >= 1
    decay = jnp.where(first, decay, jnp.ones_like(decay))
    state = jnp.where(first, state, jnp.zeros_like(state))
    distance = 1
    while distance < devices:
        earlier_decay, earlier_state = shifted((decay, state), distance)
        reached = mine >= distance
        new_decay = earlier_decay * decay
        new_state = decay[:, None, None] * earlier_state + state
        decay = jnp.where(reached, new_decay, decay)
        state = jnp.where(reached, new_state, state)
        distance *= 2
    return state


def flash_one_head_t(query_t, pair_t, key_block=4096):
    width, row_count = query_t.shape
    key_count = pair_t.shape[2]
    steps = key_count // key_block
    scale = 1.0 / math.sqrt(width)

    def kernel(q_ref, k_ref, v_ref, o_ref, top_ref, sum_ref, acc_ref):
        step = pl.program_id(0)

        @pl.when(step == 0)
        def _():
            top_ref[...] = jnp.full(top_ref.shape, -jnp.inf, jnp.float32)
            sum_ref[...] = jnp.zeros(sum_ref.shape, jnp.float32)
            acc_ref[...] = jnp.zeros(acc_ref.shape, jnp.float32)

        scores = lax.dot_general(
            k_ref[...], q_ref[...], (((0,), (0,)), ((), ())), preferred_element_type=jnp.float32
        ) * scale
        old_top = top_ref[...]
        new_top = jnp.maximum(old_top, jnp.max(scores, axis=0, keepdims=True))
        shrink = jnp.exp(old_top - new_top)
        raised = jnp.exp(scores - new_top)
        sum_ref[...] = sum_ref[...] * shrink + jnp.sum(raised, axis=0, keepdims=True)
        acc_ref[...] = acc_ref[...] * shrink + jnp.dot(
            v_ref[...], raised.astype(jnp.bfloat16), preferred_element_type=jnp.float32
        )
        top_ref[...] = new_top

        @pl.when(step == steps - 1)
        def _():
            o_ref[...] = (acc_ref[...] / sum_ref[...]).astype(o_ref.dtype)

    return pl.pallas_call(
        kernel,
        out_shape=jax.ShapeDtypeStruct((width, row_count), jnp.bfloat16),
        grid=(steps,),
        in_specs=[
            pl.BlockSpec((width, row_count), lambda j: (0, 0)),
            pl.BlockSpec((None, width, key_block), lambda j: (0, 0, j)),
            pl.BlockSpec((None, width, key_block), lambda j: (1, 0, j)),
        ],
        out_specs=pl.BlockSpec((width, row_count), lambda j: (0, 0)),
        scratch_shapes=[
            pltpu.VMEM((1, row_count), jnp.float32),
            pltpu.VMEM((1, row_count), jnp.float32),
            pltpu.VMEM((width, row_count), jnp.float32),
        ],
        compiler_params=pltpu.CompilerParams(dimension_semantics=("arbitrary",)),
    )(query_t, pair_t, pair_t)


def slot_rank(owners_here, owner_count, group_rows):
    row_count = owners_here.shape[0]
    one_hot = (owners_here[:, None] == jnp.arange(owner_count, dtype=jnp.int32)[None, :]).astype(
        jnp.bfloat16
    )
    later_rows = lax.broadcasted_iota(jnp.int32, (row_count, row_count), 0)
    earlier_cols = lax.broadcasted_iota(jnp.int32, (row_count, row_count), 1)
    before = (
        (earlier_cols < later_rows) & (later_rows // group_rows == earlier_cols // group_rows)
    ).astype(jnp.bfloat16)
    counted = jnp.dot(before, one_hot, preferred_element_type=jnp.float32)
    return jnp.sum(counted * one_hot.astype(jnp.float32), axis=1)


def per_device(
    tokens,
    queries,
    key_rows,
    values,
    ssm_input,
    write_proj,
    read_proj,
    log_decay,
    attn_project,
    ssm_project,
    gauss_project,
    tile_owner,
):
    row_count = queries.shape[0]
    head_count = queries.shape[1] // HDIM

    def spread(part):
        split = part.reshape(part.shape[:-1] + (head_count, HDIM))
        return lax.all_to_all(split, "sb", split_axis=split.ndim - 2, concat_axis=split.ndim - 3, tiled=True)

    query_heads = spread(queries)
    pair = spread(jnp.stack([key_rows, values]))
    pair_t = pair.reshape(2, -1, HDIM).transpose(0, 2, 1)
    gathered = lax.all_gather(pair_t, ("sy", "sz"), axis=2, tiled=True)
    attended_one = flash_one_head_t(query_heads.reshape(-1, HDIM).T, gathered).T
    attended = lax.all_to_all(
        attended_one.reshape(-1, 1, HDIM), "sb", split_axis=0, concat_axis=1, tiled=True
    ).reshape(row_count, head_count * HDIM)
    cumulative, inner_part, local_state, total_decay = chain_pieces(
        ssm_input, write_proj, read_proj, log_decay
    )
    entering = pass_states(local_state, total_decay)
    ssm_mix = chain_output(cumulative, inner_part, entering, read_proj)
    owner_count = lax.axis_size("head")
    own_index = lax.axis_index("head")
    sub_rows = row_count // owner_count
    capacity = sub_rows // 2
    width_out = gauss_project.shape[1]
    slot_count = owner_count * capacity
    slot_ids = jnp.arange(slot_count, dtype=jnp.float32)
    partial = (
        jnp.dot(attended, attn_project, preferred_element_type=jnp.float32)
        + jnp.dot(ssm_mix, ssm_project, preferred_element_type=jnp.float32)
    ).astype(jnp.bfloat16)
    pieces = lax.all_to_all(
        partial.reshape(owner_count, sub_rows, partial.shape[1]),
        "head",
        split_axis=0,
        concat_axis=0,
        tiled=True,
    )
    update = jnp.sum(pieces.astype(jnp.float32), axis=0)
    own_tokens = lax.dynamic_slice_in_dim(tokens, own_index * sub_rows, sub_rows, 0)
    block_out = (own_tokens.astype(jnp.float32) + update).astype(jnp.bfloat16)
    gaussians = jnp.dot(block_out, gauss_project, preferred_element_type=jnp.float32).astype(
        jnp.bfloat16
    )
    owners_here = lax.dynamic_slice_in_dim(tile_owner, own_index * sub_rows, sub_rows, 0)
    slot_value = owners_here.astype(jnp.float32) * capacity + slot_rank(
        owners_here, owner_count, sub_rows
    )
    selector = (slot_ids[:, None] == slot_value[None, :]).astype(jnp.bfloat16)
    packed = jnp.dot(selector, gaussians, preferred_element_type=jnp.float32).astype(jnp.bfloat16)
    packed = packed.reshape(owner_count, capacity, width_out)
    received = lax.all_to_all(packed, "head", split_axis=0, concat_axis=0, tiled=True)
    tile_rows = received.reshape(1, 1, owner_count, capacity, width_out)
    return (block_out, tile_rows)


def solution(mesh):
    seq_count = mesh.shape["seq"]
    outer = math.gcd(seq_count, mesh.shape["head"])
    middle = math.gcd(seq_count // outer, 2)
    split_mesh = Mesh(
        mesh.devices.reshape(outer, middle, seq_count // outer // middle, mesh.shape["head"]),
        ("sb", "sy", "sz", "head"),
    )
    seq = ("sb", "sy", "sz")
    in_specs = (
        P(seq, None),
        P(seq, "head"),
        P(seq, "head"),
        P(seq, "head"),
        P(seq, "head"),
        P(seq, None),
        P(seq, None),
        P("head", seq),
        P("head", None),
        P("head", None),
        P(),
        P(seq),
    )
    out_specs = (P(("sb", "sy", "sz", "head"), None), P(seq, "head", None, None, None))
    return jax.shard_map(
        per_device, mesh=split_mesh, in_specs=in_specs, out_specs=out_specs, check_vma=False
    )
```

```python
import math

import jax
import jax.numpy as jnp
from jax import lax
from jax.experimental import pallas as pl
from jax.experimental.pallas import tpu as pltpu
from jax.sharding import Mesh, PartitionSpec as P

HDIM = 64


def chain_pieces(ssm_input, write_proj, read_proj, log_decay):
    row_count = write_proj.shape[0]
    head_count = log_decay.shape[0]
    head_width = ssm_input.shape[1] // head_count
    cumulative = jnp.cumsum(log_decay, axis=1)
    inputs_heads = ssm_input.reshape(row_count, head_count, head_width)
    later_rows = lax.broadcasted_iota(jnp.int32, (row_count, row_count), 0)
    earlier_cols = lax.broadcasted_iota(jnp.int32, (row_count, row_count), 1)
    log_gaps = cumulative[:, :, None] - cumulative[:, None, :]
    decays = jnp.exp(jnp.where((later_rows >= earlier_cols)[None], log_gaps, -jnp.inf))
    cross_terms = jnp.dot(read_proj, write_proj.T, preferred_element_type=jnp.float32)
    mixing = (decays * cross_terms[None]).astype(jnp.bfloat16)
    inner_part = jnp.einsum(
        "hts,shp->thp", mixing, inputs_heads, preferred_element_type=jnp.float32
    )
    tail_decay = jnp.exp(cumulative[:, -1:] - cumulative)
    tail_inputs = (inputs_heads.astype(jnp.float32) * tail_decay.T[:, :, None]).astype(jnp.bfloat16)
    local_state = jnp.einsum(
        "sn,shp->hnp", write_proj, tail_inputs, preferred_element_type=jnp.float32
    )
    total_decay = jnp.exp(cumulative[:, -1])
    return (cumulative, inner_part, local_state, total_decay)


def chain_output(cumulative, inner_part, entering, read_proj):
    entering_low = entering.astype(jnp.bfloat16)
    outer_part = jnp.einsum(
        "tn,hnp->thp", read_proj, entering_low, preferred_element_type=jnp.float32
    )
    mixture = inner_part + outer_part * jnp.exp(cumulative).T[:, :, None]
    scaled = mixture * lax.rsqrt(jnp.mean(mixture * mixture, axis=2, keepdims=True) + 1e-05)
    return scaled.reshape(scaled.shape[0], -1).astype(jnp.bfloat16)


def pass_states(local_state, total_decay):
    axis = ("sb", "sy", "sz")
    devices = lax.axis_size(axis)
    mine = lax.axis_index(axis)

    def shifted(tree, distance):
        pairs = [(j, j + distance) for j in range(devices - distance)]
        return jax.tree.map(lambda part: lax.ppermute(part, axis, pairs), tree)

    decay, state = shifted((total_decay, local_state), 1)
    first = mine >= 1
    decay = jnp.where(first, decay, jnp.ones_like(decay))
    state = jnp.where(first, state, jnp.zeros_like(state))
    distance = 1
    while distance < devices:
        earlier_decay, earlier_state = shifted((decay, state), distance)
        reached = mine >= distance
        new_decay = earlier_decay * decay
        new_state = decay[:, None, None] * earlier_state + state
        decay = jnp.where(reached, new_decay, decay)
        state = jnp.where(reached, new_state, state)
        distance *= 2
    return state


def flash_one_head_t(query_t, pair_t, key_block=4096):
    width, row_count = query_t.shape
    key_count = pair_t.shape[2]
    steps = key_count // key_block
    scale = 1.0 / math.sqrt(width)

    def kernel(q_ref, k_ref, v_ref, o_ref, top_ref, sum_ref, acc_ref):
        step = pl.program_id(0)

        @pl.when(step == 0)
        def _():
            top_ref[...] = jnp.full(top_ref.shape, -jnp.inf, jnp.float32)
            sum_ref[...] = jnp.zeros(sum_ref.shape, jnp.float32)
            acc_ref[...] = jnp.zeros(acc_ref.shape, jnp.float32)

        scores = lax.dot_general(
            k_ref[...], q_ref[...], (((0,), (0,)), ((), ())), preferred_element_type=jnp.float32
        ) * scale
        old_top = top_ref[...]
        new_top = jnp.maximum(old_top, jnp.max(scores, axis=0, keepdims=True))
        shrink = jnp.exp(old_top - new_top)
        raised = jnp.exp(scores - new_top)
        sum_ref[...] = sum_ref[...] * shrink + jnp.sum(raised, axis=0, keepdims=True)
        acc_ref[...] = acc_ref[...] * shrink + jnp.dot(
            v_ref[...], raised.astype(jnp.bfloat16), preferred_element_type=jnp.float32
        )
        top_ref[...] = new_top

        @pl.when(step == steps - 1)
        def _():
            o_ref[...] = (acc_ref[...] / sum_ref[...]).astype(o_ref.dtype)

    return pl.pallas_call(
        kernel,
        out_shape=jax.ShapeDtypeStruct((width, row_count), jnp.bfloat16),
        grid=(steps,),
        in_specs=[
            pl.BlockSpec((width, row_count), lambda j: (0, 0)),
            pl.BlockSpec((None, width, key_block), lambda j: (0, 0, j)),
            pl.BlockSpec((None, width, key_block), lambda j: (1, 0, j)),
        ],
        out_specs=pl.BlockSpec((width, row_count), lambda j: (0, 0)),
        scratch_shapes=[
            pltpu.VMEM((1, row_count), jnp.float32),
            pltpu.VMEM((1, row_count), jnp.float32),
            pltpu.VMEM((width, row_count), jnp.float32),
        ],
        compiler_params=pltpu.CompilerParams(dimension_semantics=("arbitrary",)),
    )(query_t, pair_t, pair_t)


def slot_rank(owners_here, owner_count, group_rows):
    row_count = owners_here.shape[0]
    one_hot = (owners_here[:, None] == jnp.arange(owner_count, dtype=jnp.int32)[None, :]).astype(
        jnp.bfloat16
    )
    later_rows = lax.broadcasted_iota(jnp.int32, (row_count, row_count), 0)
    earlier_cols = lax.broadcasted_iota(jnp.int32, (row_count, row_count), 1)
    before = (
        (earlier_cols < later_rows) & (later_rows // group_rows == earlier_cols // group_rows)
    ).astype(jnp.bfloat16)
    counted = jnp.dot(before, one_hot, preferred_element_type=jnp.float32)
    return jnp.sum(counted * one_hot.astype(jnp.float32), axis=1)


def per_device(
    tokens,
    queries,
    key_rows,
    values,
    ssm_input,
    write_proj,
    read_proj,
    log_decay,
    attn_project,
    ssm_project,
    gauss_project,
    tile_owner,
):
    row_count = queries.shape[0]
    head_count = queries.shape[1] // HDIM

    def spread(part):
        split = part.reshape(part.shape[:-1] + (head_count, HDIM))
        return lax.all_to_all(split, "sb", split_axis=split.ndim - 2, concat_axis=split.ndim - 3, tiled=True)

    query_heads = spread(queries)
    pair = spread(jnp.stack([key_rows, values]))
    pair_t = pair.reshape(2, -1, HDIM).transpose(0, 2, 1)
    gathered = lax.all_gather(pair_t, ("sy", "sz"), axis=2, tiled=True)
    peers = lax.axis_size("sb")
    query_t = query_heads.reshape(peers, 2, row_count // 2, HDIM).transpose(1, 3, 0, 2)
    halves = []
    for half in range(2):
        half_t = flash_one_head_t(query_t[half].reshape(HDIM, -1), gathered)
        halves.append(
            lax.all_to_all(
                half_t.T.reshape(-1, 1, HDIM), "sb", split_axis=0, concat_axis=1, tiled=True
            )
        )
    attended = jnp.concatenate(halves, axis=0).reshape(row_count, head_count * HDIM)
    cumulative, inner_part, local_state, total_decay = chain_pieces(
        ssm_input, write_proj, read_proj, log_decay
    )
    entering = pass_states(local_state, total_decay)
    ssm_mix = chain_output(cumulative, inner_part, entering, read_proj)
    owner_count = lax.axis_size("head")
    own_index = lax.axis_index("head")
    sub_rows = row_count // owner_count
    capacity = sub_rows // 2
    width_out = gauss_project.shape[1]
    slot_count = owner_count * capacity
    slot_ids = jnp.arange(slot_count, dtype=jnp.float32)
    partial = (
        jnp.dot(attended, attn_project, preferred_element_type=jnp.float32)
        + jnp.dot(ssm_mix, ssm_project, preferred_element_type=jnp.float32)
    ).astype(jnp.bfloat16)
    pieces = lax.all_to_all(
        partial.reshape(owner_count, sub_rows, partial.shape[1]),
        "head",
        split_axis=0,
        concat_axis=0,
        tiled=True,
    )
    update = jnp.sum(pieces.astype(jnp.float32), axis=0)
    own_tokens = lax.dynamic_slice_in_dim(tokens, own_index * sub_rows, sub_rows, 0)
    block_out = (own_tokens.astype(jnp.float32) + update).astype(jnp.bfloat16)
    gaussians = jnp.dot(block_out, gauss_project, preferred_element_type=jnp.float32).astype(
        jnp.bfloat16
    )
    owners_here = lax.dynamic_slice_in_dim(tile_owner, own_index * sub_rows, sub_rows, 0)
    slot_value = owners_here.astype(jnp.float32) * capacity + slot_rank(
        owners_here, owner_count, sub_rows
    )
    selector = (slot_ids[:, None] == slot_value[None, :]).astype(jnp.bfloat16)
    packed = jnp.dot(selector, gaussians, preferred_element_type=jnp.float32).astype(jnp.bfloat16)
    packed = packed.reshape(owner_count, capacity, width_out)
    received = lax.all_to_all(packed, "head", split_axis=0, concat_axis=0, tiled=True)
    tile_rows = received.reshape(1, 1, owner_count, capacity, width_out)
    return (block_out, tile_rows)


def solution(mesh):
    seq_count = mesh.shape["seq"]
    outer = math.gcd(seq_count, mesh.shape["head"])
    middle = math.gcd(seq_count // outer, 2)
    split_mesh = Mesh(
        mesh.devices.reshape(outer, middle, seq_count // outer // middle, mesh.shape["head"]),
        ("sb", "sy", "sz", "head"),
    )
    seq = ("sb", "sy", "sz")
    in_specs = (
        P(seq, None),
        P(seq, "head"),
        P(seq, "head"),
        P(seq, "head"),
        P(seq, "head"),
        P(seq, None),
        P(seq, None),
        P("head", seq),
        P("head", None),
        P("head", None),
        P(),
        P(seq),
    )
    out_specs = (P(("sb", "sy", "sz", "head"), None), P(seq, "head", None, None, None))
    return jax.shard_map(
        per_device, mesh=split_mesh, in_specs=in_specs, out_specs=out_specs, check_vma=False
    )
```

```python
import math

import jax
import jax.numpy as jnp
from jax import lax
from jax.experimental import pallas as pl
from jax.experimental.pallas import tpu as pltpu
from jax.sharding import Mesh, PartitionSpec as P

HDIM = 64


def chain_pieces(ssm_input, write_proj, read_proj, log_decay):
    row_count = write_proj.shape[0]
    head_count = log_decay.shape[0]
    head_width = ssm_input.shape[1] // head_count
    cumulative = jnp.cumsum(log_decay, axis=1)
    inputs_heads = ssm_input.reshape(row_count, head_count, head_width)
    later_rows = lax.broadcasted_iota(jnp.int32, (row_count, row_count), 0)
    earlier_cols = lax.broadcasted_iota(jnp.int32, (row_count, row_count), 1)
    log_gaps = cumulative[:, :, None] - cumulative[:, None, :]
    decays = jnp.exp(jnp.where((later_rows >= earlier_cols)[None], log_gaps, -jnp.inf))
    cross_terms = jnp.dot(read_proj, write_proj.T, preferred_element_type=jnp.float32)
    mixing = (decays * cross_terms[None]).astype(jnp.bfloat16)
    inner_part = jnp.einsum(
        "hts,shp->thp", mixing, inputs_heads, preferred_element_type=jnp.float32
    )
    tail_decay = jnp.exp(cumulative[:, -1:] - cumulative)
    tail_inputs = (inputs_heads.astype(jnp.float32) * tail_decay.T[:, :, None]).astype(jnp.bfloat16)
    local_state = jnp.einsum(
        "sn,shp->hnp", write_proj, tail_inputs, preferred_element_type=jnp.float32
    )
    total_decay = jnp.exp(cumulative[:, -1])
    return (cumulative, inner_part, local_state, total_decay)


def chain_output(cumulative, inner_part, entering, read_proj):
    entering_low = entering.astype(jnp.bfloat16)
    outer_part = jnp.einsum(
        "tn,hnp->thp", read_proj, entering_low, preferred_element_type=jnp.float32
    )
    mixture = inner_part + outer_part * jnp.exp(cumulative).T[:, :, None]
    scaled = mixture * lax.rsqrt(jnp.mean(mixture * mixture, axis=2, keepdims=True) + 1e-05)
    return scaled.reshape(scaled.shape[0], -1).astype(jnp.bfloat16)


def pass_states(local_state, total_decay):
    axis = ("sb", "sy", "sz")
    devices = lax.axis_size(axis)
    mine = lax.axis_index(axis)

    def shifted(tree, distance):
        pairs = [(j, j + distance) for j in range(devices - distance)]
        return jax.tree.map(
            lambda part: lax.ppermute(
                part.astype(jnp.bfloat16) if part.ndim == 3 else part, axis, pairs
            ).astype(part.dtype),
            tree,
        )

    decay, state = shifted((total_decay, local_state), 1)
    first = mine >= 1
    decay = jnp.where(first, decay, jnp.ones_like(decay))
    state = jnp.where(first, state, jnp.zeros_like(state))
    distance = 1
    while distance < devices:
        earlier_decay, earlier_state = shifted((decay, state), distance)
        reached = mine >= distance
        new_decay = earlier_decay * decay
        new_state = decay[:, None, None] * earlier_state + state
        decay = jnp.where(reached, new_decay, decay)
        state = jnp.where(reached, new_state, state)
        distance *= 2
    return state


def flash_one_head_t(query_t, pair_t, key_block=4096):
    width, row_count = query_t.shape
    key_count = pair_t.shape[2]
    steps = key_count // key_block
    scale = 1.0 / math.sqrt(width)

    def kernel(q_ref, k_ref, v_ref, o_ref, top_ref, sum_ref, acc_ref):
        step = pl.program_id(0)

        @pl.when(step == 0)
        def _():
            top_ref[...] = jnp.full(top_ref.shape, -jnp.inf, jnp.float32)
            sum_ref[...] = jnp.zeros(sum_ref.shape, jnp.float32)
            acc_ref[...] = jnp.zeros(acc_ref.shape, jnp.float32)

        scores = lax.dot_general(
            k_ref[...], q_ref[...], (((0,), (0,)), ((), ())), preferred_element_type=jnp.float32
        ) * scale
        old_top = top_ref[...]
        new_top = jnp.maximum(old_top, jnp.max(scores, axis=0, keepdims=True))
        shrink = jnp.exp(old_top - new_top)
        raised = jnp.exp(scores - new_top)
        sum_ref[...] = sum_ref[...] * shrink + jnp.sum(raised, axis=0, keepdims=True)
        acc_ref[...] = acc_ref[...] * shrink + jnp.dot(
            v_ref[...], raised.astype(jnp.bfloat16), preferred_element_type=jnp.float32
        )
        top_ref[...] = new_top

        @pl.when(step == steps - 1)
        def _():
            o_ref[...] = (acc_ref[...] / sum_ref[...]).astype(o_ref.dtype)

    return pl.pallas_call(
        kernel,
        out_shape=jax.ShapeDtypeStruct((width, row_count), jnp.bfloat16),
        grid=(steps,),
        in_specs=[
            pl.BlockSpec((width, row_count), lambda j: (0, 0)),
            pl.BlockSpec((None, width, key_block), lambda j: (0, 0, j)),
            pl.BlockSpec((None, width, key_block), lambda j: (1, 0, j)),
        ],
        out_specs=pl.BlockSpec((width, row_count), lambda j: (0, 0)),
        scratch_shapes=[
            pltpu.VMEM((1, row_count), jnp.float32),
            pltpu.VMEM((1, row_count), jnp.float32),
            pltpu.VMEM((width, row_count), jnp.float32),
        ],
        compiler_params=pltpu.CompilerParams(dimension_semantics=("arbitrary",)),
    )(query_t, pair_t, pair_t)


def slot_rank(owners_here, owner_count, group_rows):
    row_count = owners_here.shape[0]
    one_hot = (owners_here[:, None] == jnp.arange(owner_count, dtype=jnp.int32)[None, :]).astype(
        jnp.bfloat16
    )
    later_rows = lax.broadcasted_iota(jnp.int32, (row_count, row_count), 0)
    earlier_cols = lax.broadcasted_iota(jnp.int32, (row_count, row_count), 1)
    before = (
        (earlier_cols < later_rows) & (later_rows // group_rows == earlier_cols // group_rows)
    ).astype(jnp.bfloat16)
    counted = jnp.dot(before, one_hot, preferred_element_type=jnp.float32)
    return jnp.sum(counted * one_hot.astype(jnp.float32), axis=1)


def per_device(
    tokens,
    queries,
    key_rows,
    values,
    ssm_input,
    write_proj,
    read_proj,
    log_decay,
    attn_project,
    ssm_project,
    gauss_project,
    tile_owner,
):
    row_count = queries.shape[0]
    head_count = queries.shape[1] // HDIM

    def spread(part):
        split = part.reshape(part.shape[:-1] + (head_count, HDIM))
        return lax.all_to_all(split, "sb", split_axis=split.ndim - 2, concat_axis=split.ndim - 3, tiled=True)

    query_heads = spread(queries)
    pair = spread(jnp.stack([key_rows, values]))
    pair_t = pair.reshape(2, -1, HDIM).transpose(0, 2, 1)
    gathered = lax.all_gather(pair_t, ("sy", "sz"), axis=2, tiled=True)
    attended_one = flash_one_head_t(query_heads.reshape(-1, HDIM).T, gathered).T
    attended = lax.all_to_all(
        attended_one.reshape(-1, 1, HDIM), "sb", split_axis=0, concat_axis=1, tiled=True
    ).reshape(row_count, head_count * HDIM)
    cumulative, inner_part, local_state, total_decay = chain_pieces(
        ssm_input, write_proj, read_proj, log_decay
    )
    entering = pass_states(local_state, total_decay)
    ssm_mix = chain_output(cumulative, inner_part, entering, read_proj)
    owner_count = lax.axis_size("head")
    own_index = lax.axis_index("head")
    sub_rows = row_count // owner_count
    capacity = sub_rows // 2
    width_out = gauss_project.shape[1]
    slot_count = owner_count * capacity
    slot_ids = jnp.arange(slot_count, dtype=jnp.float32)
    partial = (
        jnp.dot(attended, attn_project, preferred_element_type=jnp.float32)
        + jnp.dot(ssm_mix, ssm_project, preferred_element_type=jnp.float32)
    ).astype(jnp.bfloat16)
    pieces = lax.all_to_all(
        partial.reshape(owner_count, sub_rows, partial.shape[1]),
        "head",
        split_axis=0,
        concat_axis=0,
        tiled=True,
    )
    update = jnp.sum(pieces.astype(jnp.float32), axis=0)
    own_tokens = lax.dynamic_slice_in_dim(tokens, own_index * sub_rows, sub_rows, 0)
    block_out = (own_tokens.astype(jnp.float32) + update).astype(jnp.bfloat16)
    gaussians = jnp.dot(block_out, gauss_project, preferred_element_type=jnp.float32).astype(
        jnp.bfloat16
    )
    owners_here = lax.dynamic_slice_in_dim(tile_owner, own_index * sub_rows, sub_rows, 0)
    slot_value = owners_here.astype(jnp.float32) * capacity + slot_rank(
        owners_here, owner_count, sub_rows
    )
    selector = (slot_ids[:, None] == slot_value[None, :]).astype(jnp.bfloat16)
    packed = jnp.dot(selector, gaussians, preferred_element_type=jnp.float32).astype(jnp.bfloat16)
    packed = packed.reshape(owner_count, capacity, width_out)
    received = lax.all_to_all(packed, "head", split_axis=0, concat_axis=0, tiled=True)
    tile_rows = received.reshape(1, 1, owner_count, capacity, width_out)
    return (block_out, tile_rows)


def solution(mesh):
    seq_count = mesh.shape["seq"]
    outer = math.gcd(seq_count, mesh.shape["head"])
    middle = math.gcd(seq_count // outer, 2)
    split_mesh = Mesh(
        mesh.devices.reshape(outer, middle, seq_count // outer // middle, mesh.shape["head"]),
        ("sb", "sy", "sz", "head"),
    )
    seq = ("sb", "sy", "sz")
    in_specs = (
        P(seq, None),
        P(seq, "head"),
        P(seq, "head"),
        P(seq, "head"),
        P(seq, "head"),
        P(seq, None),
        P(seq, None),
        P("head", seq),
        P("head", None),
        P("head", None),
        P(),
        P(seq),
    )
    out_specs = (P(("sb", "sy", "sz", "head"), None), P(seq, "head", None, None, None))
    return jax.shard_map(
        per_device, mesh=split_mesh, in_specs=in_specs, out_specs=out_specs, check_vma=False
    )
```

```python
import math

import jax
import jax.numpy as jnp
from jax import lax
from jax.experimental import pallas as pl
from jax.experimental.pallas import tpu as pltpu
from jax.sharding import Mesh, PartitionSpec as P

HDIM = 64


def chain_pieces(ssm_input, write_proj, read_proj, log_decay):
    row_count = write_proj.shape[0]
    head_count = log_decay.shape[0]
    head_width = ssm_input.shape[1] // head_count
    cumulative = jnp.cumsum(log_decay, axis=1)
    inputs_heads = ssm_input.reshape(row_count, head_count, head_width)
    later_rows = lax.broadcasted_iota(jnp.int32, (row_count, row_count), 0)
    earlier_cols = lax.broadcasted_iota(jnp.int32, (row_count, row_count), 1)
    log_gaps = cumulative[:, :, None] - cumulative[:, None, :]
    decays = jnp.exp(jnp.where((later_rows >= earlier_cols)[None], log_gaps, -jnp.inf))
    cross_terms = jnp.dot(read_proj, write_proj.T, preferred_element_type=jnp.float32)
    mixing = (decays * cross_terms[None]).astype(jnp.bfloat16)
    inner_part = jnp.einsum(
        "hts,shp->thp", mixing, inputs_heads, preferred_element_type=jnp.float32
    )
    tail_decay = jnp.exp(cumulative[:, -1:] - cumulative)
    tail_inputs = (inputs_heads.astype(jnp.float32) * tail_decay.T[:, :, None]).astype(jnp.bfloat16)
    local_state = jnp.einsum(
        "sn,shp->hnp", write_proj, tail_inputs, preferred_element_type=jnp.float32
    )
    total_decay = jnp.exp(cumulative[:, -1])
    return (cumulative, inner_part, local_state, total_decay)


def chain_output(cumulative, inner_part, entering, read_proj):
    entering_low = entering.astype(jnp.bfloat16)
    outer_part = jnp.einsum(
        "tn,hnp->thp", read_proj, entering_low, preferred_element_type=jnp.float32
    )
    mixture = inner_part + outer_part * jnp.exp(cumulative).T[:, :, None]
    scaled = mixture * lax.rsqrt(jnp.mean(mixture * mixture, axis=2, keepdims=True) + 1e-05)
    return scaled.reshape(scaled.shape[0], -1).astype(jnp.bfloat16)


def pass_states(local_state, total_decay):
    axis = ("sx", "sy", "sh", "sz")
    devices = lax.axis_size(axis)
    mine = lax.axis_index(axis)

    def shifted(tree, distance):
        pairs = [(j, j + distance) for j in range(devices - distance)]
        return jax.tree.map(
            lambda part: lax.ppermute(
                part.astype(jnp.bfloat16) if part.ndim == 3 else part, axis, pairs
            ).astype(part.dtype),
            tree,
        )

    decay, state = shifted((total_decay, local_state), 1)
    first = mine >= 1
    decay = jnp.where(first, decay, jnp.ones_like(decay))
    state = jnp.where(first, state, jnp.zeros_like(state))
    distance = 1
    while distance < devices:
        earlier_decay, earlier_state = shifted((decay, state), distance)
        reached = mine >= distance
        new_decay = earlier_decay * decay
        new_state = decay[:, None, None] * earlier_state + state
        decay = jnp.where(reached, new_decay, decay)
        state = jnp.where(reached, new_state, state)
        distance *= 2
    return state


def flash_one_head_t(query_t, pair_t, key_block=4096):
    width, row_count = query_t.shape
    key_count = pair_t.shape[2]
    steps = key_count // key_block
    scale = 1.0 / math.sqrt(width)

    def kernel(q_ref, k_ref, v_ref, o_ref, top_ref, sum_ref, acc_ref):
        step = pl.program_id(0)

        @pl.when(step == 0)
        def _():
            top_ref[...] = jnp.full(top_ref.shape, -jnp.inf, jnp.float32)
            sum_ref[...] = jnp.zeros(sum_ref.shape, jnp.float32)
            acc_ref[...] = jnp.zeros(acc_ref.shape, jnp.float32)

        scores = lax.dot_general(
            k_ref[...], q_ref[...], (((0,), (0,)), ((), ())), preferred_element_type=jnp.float32
        ) * scale
        old_top = top_ref[...]
        new_top = jnp.maximum(old_top, jnp.max(scores, axis=0, keepdims=True))
        shrink = jnp.exp(old_top - new_top)
        raised = jnp.exp(scores - new_top)
        sum_ref[...] = sum_ref[...] * shrink + jnp.sum(raised, axis=0, keepdims=True)
        acc_ref[...] = acc_ref[...] * shrink + jnp.dot(
            v_ref[...], raised.astype(jnp.bfloat16), preferred_element_type=jnp.float32
        )
        top_ref[...] = new_top

        @pl.when(step == steps - 1)
        def _():
            o_ref[...] = (acc_ref[...] / sum_ref[...]).astype(o_ref.dtype)

    return pl.pallas_call(
        kernel,
        out_shape=jax.ShapeDtypeStruct((width, row_count), jnp.bfloat16),
        grid=(steps,),
        in_specs=[
            pl.BlockSpec((width, row_count), lambda j: (0, 0)),
            pl.BlockSpec((None, width, key_block), lambda j: (0, 0, j)),
            pl.BlockSpec((None, width, key_block), lambda j: (1, 0, j)),
        ],
        out_specs=pl.BlockSpec((width, row_count), lambda j: (0, 0)),
        scratch_shapes=[
            pltpu.VMEM((1, row_count), jnp.float32),
            pltpu.VMEM((1, row_count), jnp.float32),
            pltpu.VMEM((width, row_count), jnp.float32),
        ],
        compiler_params=pltpu.CompilerParams(dimension_semantics=("arbitrary",)),
    )(query_t, pair_t, pair_t)


def slot_rank(owners_here, owner_count, group_rows):
    row_count = owners_here.shape[0]
    one_hot = (owners_here[:, None] == jnp.arange(owner_count, dtype=jnp.int32)[None, :]).astype(
        jnp.bfloat16
    )
    later_rows = lax.broadcasted_iota(jnp.int32, (row_count, row_count), 0)
    earlier_cols = lax.broadcasted_iota(jnp.int32, (row_count, row_count), 1)
    before = (
        (earlier_cols < later_rows) & (later_rows // group_rows == earlier_cols // group_rows)
    ).astype(jnp.bfloat16)
    counted = jnp.dot(before, one_hot, preferred_element_type=jnp.float32)
    return jnp.sum(counted * one_hot.astype(jnp.float32), axis=1)


def per_device(
    tokens,
    queries,
    key_rows,
    values,
    ssm_input,
    write_proj,
    read_proj,
    log_decay,
    attn_project,
    ssm_project,
    gauss_project,
    tile_owner,
):
    row_count = queries.shape[0]
    head_count = queries.shape[1] // HDIM

    def spread(part):
        split = part.reshape(part.shape[:-1] + (head_count, HDIM))
        return lax.all_to_all(split, ("sy", "sh"), split_axis=split.ndim - 2, concat_axis=split.ndim - 3, tiled=True)

    query_heads = spread(queries)
    pair = spread(jnp.stack([key_rows, values]))
    pair_t = pair.reshape(2, -1, HDIM).transpose(0, 2, 1)
    gathered = lax.all_gather(pair_t, ("sx", "sz"), axis=2, tiled=True)
    attended_one = flash_one_head_t(query_heads.reshape(-1, HDIM).T, gathered).T
    attended = lax.all_to_all(
        attended_one.reshape(-1, 1, HDIM), ("sy", "sh"), split_axis=0, concat_axis=1, tiled=True
    ).reshape(row_count, head_count * HDIM)
    cumulative, inner_part, local_state, total_decay = chain_pieces(
        ssm_input, write_proj, read_proj, log_decay
    )
    entering = pass_states(local_state, total_decay)
    ssm_mix = chain_output(cumulative, inner_part, entering, read_proj)
    owner_count = lax.axis_size("head")
    own_index = lax.axis_index("head")
    sub_rows = row_count // owner_count
    capacity = sub_rows // 2
    width_out = gauss_project.shape[1]
    slot_count = owner_count * capacity
    slot_ids = jnp.arange(slot_count, dtype=jnp.float32)
    partial = (
        jnp.dot(attended, attn_project, preferred_element_type=jnp.float32)
        + jnp.dot(ssm_mix, ssm_project, preferred_element_type=jnp.float32)
    ).astype(jnp.bfloat16)
    pieces = lax.all_to_all(
        partial.reshape(owner_count, sub_rows, partial.shape[1]),
        "head",
        split_axis=0,
        concat_axis=0,
        tiled=True,
    )
    update = jnp.sum(pieces.astype(jnp.float32), axis=0)
    own_tokens = lax.dynamic_slice_in_dim(tokens, own_index * sub_rows, sub_rows, 0)
    block_out = (own_tokens.astype(jnp.float32) + update).astype(jnp.bfloat16)
    gaussians = jnp.dot(block_out, gauss_project, preferred_element_type=jnp.float32).astype(
        jnp.bfloat16
    )
    owners_here = lax.dynamic_slice_in_dim(tile_owner, own_index * sub_rows, sub_rows, 0)
    slot_value = owners_here.astype(jnp.float32) * capacity + slot_rank(
        owners_here, owner_count, sub_rows
    )
    selector = (slot_ids[:, None] == slot_value[None, :]).astype(jnp.bfloat16)
    packed = jnp.dot(selector, gaussians, preferred_element_type=jnp.float32).astype(jnp.bfloat16)
    packed = packed.reshape(owner_count, capacity, width_out)
    received = lax.all_to_all(packed, "head", split_axis=0, concat_axis=0, tiled=True)
    tile_rows = received.reshape(1, 1, owner_count, capacity, width_out)
    return (block_out, tile_rows)


def solution(mesh):
    seq_count = mesh.shape["seq"]
    outer = math.gcd(seq_count, mesh.shape["head"])
    split_mesh = Mesh(
        mesh.devices.reshape(outer, 2, 2, seq_count // outer // 4, mesh.shape["head"]),
        ("sx", "sy", "sh", "sz", "head"),
    )
    seq = ("sx", "sy", "sh", "sz")
    in_specs = (
        P(seq, None),
        P(seq, "head"),
        P(seq, "head"),
        P(seq, "head"),
        P(seq, "head"),
        P(seq, None),
        P(seq, None),
        P("head", seq),
        P("head", None),
        P("head", None),
        P(),
        P(seq),
    )
    out_specs = (P(("sx", "sy", "sh", "sz", "head"), None), P(seq, "head", None, None, None))
    return jax.shard_map(
        per_device, mesh=split_mesh, in_specs=in_specs, out_specs=out_specs, check_vma=False
    )
```

```python
import math

import jax
import jax.numpy as jnp
from jax import lax
from jax.experimental import pallas as pl
from jax.experimental.pallas import tpu as pltpu
from jax.sharding import Mesh, PartitionSpec as P

HDIM = 64


def chain_pieces(ssm_input, write_proj, read_proj, log_decay):
    row_count = write_proj.shape[0]
    head_count = log_decay.shape[0]
    head_width = ssm_input.shape[1] // head_count
    cumulative = jnp.cumsum(log_decay, axis=1)
    inputs_heads = ssm_input.reshape(row_count, head_count, head_width)
    later_rows = lax.broadcasted_iota(jnp.int32, (row_count, row_count), 0)
    earlier_cols = lax.broadcasted_iota(jnp.int32, (row_count, row_count), 1)
    log_gaps = cumulative[:, :, None] - cumulative[:, None, :]
    decays = jnp.exp(jnp.where((later_rows >= earlier_cols)[None], log_gaps, -jnp.inf))
    cross_terms = jnp.dot(read_proj, write_proj.T, preferred_element_type=jnp.float32)
    mixing = (decays * cross_terms[None]).astype(jnp.bfloat16)
    inner_part = jnp.einsum(
        "hts,shp->thp", mixing, inputs_heads, preferred_element_type=jnp.float32
    )
    tail_decay = jnp.exp(cumulative[:, -1:] - cumulative)
    tail_inputs = (inputs_heads.astype(jnp.float32) * tail_decay.T[:, :, None]).astype(jnp.bfloat16)
    local_state = jnp.einsum(
        "sn,shp->hnp", write_proj, tail_inputs, preferred_element_type=jnp.float32
    )
    total_decay = jnp.exp(cumulative[:, -1])
    return (cumulative, inner_part, local_state, total_decay)


def chain_output(cumulative, inner_part, entering, read_proj):
    entering_low = entering.astype(jnp.bfloat16)
    outer_part = jnp.einsum(
        "tn,hnp->thp", read_proj, entering_low, preferred_element_type=jnp.float32
    )
    mixture = inner_part + outer_part * jnp.exp(cumulative).T[:, :, None]
    scaled = mixture * lax.rsqrt(jnp.mean(mixture * mixture, axis=2, keepdims=True) + 1e-05)
    return scaled.reshape(scaled.shape[0], -1).astype(jnp.bfloat16)


def pass_states(local_state, total_decay):
    axis = ("sb", "sy", "sz")
    devices = lax.axis_size(axis)
    mine = lax.axis_index(axis)

    def shifted(tree, distance):
        pairs = [(j, j + distance) for j in range(devices - distance)]
        return jax.tree.map(
            lambda part: lax.ppermute(
                part.astype(jnp.bfloat16) if part.ndim == 3 else part, axis, pairs
            ).astype(part.dtype),
            tree,
        )

    decay, state = shifted((total_decay, local_state), 1)
    first = mine >= 1
    decay = jnp.where(first, decay, jnp.ones_like(decay))
    state = jnp.where(first, state, jnp.zeros_like(state))
    distance = 1
    while distance < devices:
        earlier_decay, earlier_state = shifted((decay, state), distance)
        reached = mine >= distance
        new_decay = earlier_decay * decay
        new_state = decay[:, None, None] * earlier_state + state
        decay = jnp.where(reached, new_decay, decay)
        state = jnp.where(reached, new_state, state)
        distance *= 2
    return state


def flash_one_head_t(query_t, pair_t, key_block=4096):
    width, row_count = query_t.shape
    key_count = pair_t.shape[2]
    steps = key_count // key_block
    scale = 1.0 / math.sqrt(width)

    def kernel(q_ref, k_ref, v_ref, o_ref, top_ref, sum_ref, acc_ref):
        step = pl.program_id(0)

        @pl.when(step == 0)
        def _():
            top_ref[...] = jnp.full(top_ref.shape, -jnp.inf, jnp.float32)
            sum_ref[...] = jnp.zeros(sum_ref.shape, jnp.float32)
            acc_ref[...] = jnp.zeros(acc_ref.shape, jnp.float32)

        scores = lax.dot_general(
            k_ref[...], q_ref[...], (((0,), (0,)), ((), ())), preferred_element_type=jnp.float32
        ) * scale
        old_top = top_ref[...]
        new_top = jnp.maximum(old_top, jnp.max(scores, axis=0, keepdims=True))
        shrink = jnp.exp(old_top - new_top)
        raised = jnp.exp(scores - new_top)
        sum_ref[...] = sum_ref[...] * shrink + jnp.sum(raised, axis=0, keepdims=True)
        acc_ref[...] = acc_ref[...] * shrink + jnp.dot(
            v_ref[...], raised.astype(jnp.bfloat16), preferred_element_type=jnp.float32
        )
        top_ref[...] = new_top

        @pl.when(step == steps - 1)
        def _():
            o_ref[...] = (acc_ref[...] / sum_ref[...]).astype(o_ref.dtype)

    return pl.pallas_call(
        kernel,
        out_shape=jax.ShapeDtypeStruct((width, row_count), jnp.bfloat16),
        grid=(steps,),
        in_specs=[
            pl.BlockSpec((width, row_count), lambda j: (0, 0)),
            pl.BlockSpec((None, width, key_block), lambda j: (0, 0, j)),
            pl.BlockSpec((None, width, key_block), lambda j: (1, 0, j)),
        ],
        out_specs=pl.BlockSpec((width, row_count), lambda j: (0, 0)),
        scratch_shapes=[
            pltpu.VMEM((1, row_count), jnp.float32),
            pltpu.VMEM((1, row_count), jnp.float32),
            pltpu.VMEM((width, row_count), jnp.float32),
        ],
        compiler_params=pltpu.CompilerParams(dimension_semantics=("arbitrary",)),
    )(query_t, pair_t, pair_t)


def slot_rank(owners_here, owner_count, group_rows):
    row_count = owners_here.shape[0]
    one_hot = (owners_here[:, None] == jnp.arange(owner_count, dtype=jnp.int32)[None, :]).astype(
        jnp.bfloat16
    )
    later_rows = lax.broadcasted_iota(jnp.int32, (row_count, row_count), 0)
    earlier_cols = lax.broadcasted_iota(jnp.int32, (row_count, row_count), 1)
    before = (
        (earlier_cols < later_rows) & (later_rows // group_rows == earlier_cols // group_rows)
    ).astype(jnp.bfloat16)
    counted = jnp.dot(before, one_hot, preferred_element_type=jnp.float32)
    return jnp.sum(counted * one_hot.astype(jnp.float32), axis=1)


def per_device(
    tokens,
    queries,
    key_rows,
    values,
    ssm_input,
    write_proj,
    read_proj,
    log_decay,
    attn_project,
    ssm_project,
    gauss_project,
    tile_owner,
):
    row_count = queries.shape[0]
    head_count = queries.shape[1] // HDIM

    def spread(part):
        split = part.reshape(part.shape[:-1] + (head_count, HDIM))
        return lax.all_to_all(split, "sb", split_axis=split.ndim - 2, concat_axis=split.ndim - 3, tiled=True)

    query_heads = spread(queries)
    pair = spread(jnp.stack([key_rows, values]))
    pair_t = pair.reshape(2, -1, HDIM).transpose(0, 2, 1)
    gathered = lax.all_gather(pair_t, ("sy", "sz"), axis=2, tiled=True)
    cumulative, inner_part, local_state, total_decay = chain_pieces(
        ssm_input, write_proj, read_proj, log_decay
    )
    entering = pass_states(local_state, total_decay)
    ssm_mix = chain_output(cumulative, inner_part, entering, read_proj)
    ssm_part = jnp.dot(ssm_mix, ssm_project, preferred_element_type=jnp.float32)
    gathered, ssm_part = lax.optimization_barrier((gathered, ssm_part))
    attended_one = flash_one_head_t(query_heads.reshape(-1, HDIM).T, gathered).T
    attended = lax.all_to_all(
        attended_one.reshape(-1, 1, HDIM), "sb", split_axis=0, concat_axis=1, tiled=True
    ).reshape(row_count, head_count * HDIM)
    owner_count = lax.axis_size("head")
    own_index = lax.axis_index("head")
    sub_rows = row_count // owner_count
    capacity = sub_rows // 2
    width_out = gauss_project.shape[1]
    slot_count = owner_count * capacity
    slot_ids = jnp.arange(slot_count, dtype=jnp.float32)
    partial = (
        jnp.dot(attended, attn_project, preferred_element_type=jnp.float32)
        + ssm_part
    ).astype(jnp.bfloat16)
    pieces = lax.all_to_all(
        partial.reshape(owner_count, sub_rows, partial.shape[1]),
        "head",
        split_axis=0,
        concat_axis=0,
        tiled=True,
    )
    update = jnp.sum(pieces.astype(jnp.float32), axis=0)
    own_tokens = lax.dynamic_slice_in_dim(tokens, own_index * sub_rows, sub_rows, 0)
    block_out = (own_tokens.astype(jnp.float32) + update).astype(jnp.bfloat16)
    gaussians = jnp.dot(block_out, gauss_project, preferred_element_type=jnp.float32).astype(
        jnp.bfloat16
    )
    owners_here = lax.dynamic_slice_in_dim(tile_owner, own_index * sub_rows, sub_rows, 0)
    slot_value = owners_here.astype(jnp.float32) * capacity + slot_rank(
        owners_here, owner_count, sub_rows
    )
    selector = (slot_ids[:, None] == slot_value[None, :]).astype(jnp.bfloat16)
    packed = jnp.dot(selector, gaussians, preferred_element_type=jnp.float32).astype(jnp.bfloat16)
    packed = packed.reshape(owner_count, capacity, width_out)
    received = lax.all_to_all(packed, "head", split_axis=0, concat_axis=0, tiled=True)
    tile_rows = received.reshape(1, 1, owner_count, capacity, width_out)
    return (block_out, tile_rows)


def solution(mesh):
    seq_count = mesh.shape["seq"]
    outer = math.gcd(seq_count, mesh.shape["head"])
    middle = math.gcd(seq_count // outer, 2)
    split_mesh = Mesh(
        mesh.devices.reshape(outer, middle, seq_count // outer // middle, mesh.shape["head"]),
        ("sb", "sy", "sz", "head"),
    )
    seq = ("sb", "sy", "sz")
    in_specs = (
        P(seq, None),
        P(seq, "head"),
        P(seq, "head"),
        P(seq, "head"),
        P(seq, "head"),
        P(seq, None),
        P(seq, None),
        P("head", seq),
        P("head", None),
        P("head", None),
        P(),
        P(seq),
    )
    out_specs = (P(("sb", "sy", "sz", "head"), None), P(seq, "head", None, None, None))
    return jax.shard_map(
        per_device, mesh=split_mesh, in_specs=in_specs, out_specs=out_specs, check_vma=False
    )
```
